32 devices in a mesh: groups: 2 (over x), tiles: 16 (over z, y, core).
Axes of the slice: x: 2, y: 2, z: 4, core: 2. Of those that a mesh axis runs over, the one named last changes fastest.
Arguments:
- coeffs: float32 [8192, 16384], P(('groups', 'tiles')), parts along dimension 0, may hold values from -0.09375 to 0.09375
- occupation: float32 [8192], P(('groups', 'tiles')), parts along dimension 0, may hold values from -1 to 1
- kept_tiles: int32 [64, 2], P('groups'), parts along dimension 0, may hold values from 0 to 255, as said below
- tile_slot: int32 [64], P('groups'), parts along dimension 0, may hold values from 0 to 31, as said below
- blocks: int32 [256, 8], P('groups'), parts along dimension 0, may hold values from 0 to 255, as said below
- batch_slot: int32 [256], P('groups'), parts along dimension 0, may hold values from 0 to 127, as said below
- tables: float32 [256, 512, 256], P(('groups', 'tiles')), parts along dimension 0, may hold values from -3.6 to 3.6
- weights: float32 [256, 256], P(('groups', 'tiles')), parts along dimension 0, may hold values from 0.005 to 0.05
- local_pot: float32 [256, 256], P(('groups', 'tiles')), parts along dimension 0, may hold values from -6 to 6
Outputs:
- density: float32 [256, 256], P(('groups', 'tiles')), parts along dimension 0
- matrix: float32 [64, 4096], P(('groups', 'tiles')), parts along dimension 0
The draws below stay inside these ranges and needn't reach their ends.
There are 2 independent parts, one for each index of `groups`. The reference program is written for one: setup_inputs(seed, part) draws one part's arguments, and reference() takes and returns one part's arrays. A program takes and returns all parts, laid end to end along the dimension named above; each array names one. Nothing has to cross between parts.
Inputs may be any that keep to these rules, and one draw needn't show every extreme that they name: `kept_tiles`: distinct pairs (row block, column block). A permutation; slot tile_slot[k] is held by the device of index tile_slot[k] // 2 along tiles. Of the kept tiles that lie within the blocks of the batches held by one device, at most 2 are held by any one device. Each row names 8 different blocks. The devices come in aligned block clusters of 4 (indices 0 to 3, and so on); all batches held by the devices of one cluster name the same blocks, each batch in an order of its own, and different clusters name disjoint blocks. At most 16 kept tiles lie within the blocks of one batch. A permutation; the tables, weights, potential and density of batch b sit at slot batch_slot[b], held by the device of index batch_slot[b] // 8.
All inputs are finite; a program needn't handle non-finite values.
Results may differ from the reference program's by a relative error of at most 0.0003.
Values sent between devices are 32-bit elements; how exact they have to be, the bound alone decides.
No kernel may reach another device: no remote copies, remote signals or barrier semaphores. Data moves between devices by JAX's collectives and lax.ppermute only.
A program may use at most 128 MiB of HBM per device.

```python
import math
import jax
import jax.numpy as jnp
from jax import lax

NB = 16384
NS = 4096
BS = 64
OV = 8
PTS = 256
DEV_CL = 4
KT_DEV = 2
BAT_DEV = 8
NBLK = 256
NBAT = 128
KEPT = 32
NCL = 4
NEEDB = 16


def layout(key):
    base_key = jax.random.fold_in(key, 4099)
    streams = jax.random.split(base_key, 8)
    holders = KEPT // KT_DEV
    block_order = jax.random.permutation(streams[0], NBLK).astype(jnp.int32)
    cluster_blocks = block_order[:NCL * OV].reshape(NCL, OV)
    largest = jax.random.randint(streams[1], (), 0, NCL)
    others = NCL - 1
    spread_total = KEPT - NEEDB
    even_share = spread_total // others
    remainder = spread_total % others
    ladder = jnp.arange(others, dtype=jnp.int32)
    counts = even_share + (ladder < remainder).astype(jnp.int32)
    raw_draws = jax.random.randint(streams[2], (others,), 0, 1 << 20)
    moved_count = jnp.where((ladder % 2 == 0) & (ladder + 1 < others), raw_draws % counts, 0)
    counts = counts - moved_count + jnp.roll(moved_count, 1)
    cluster_ladder = jnp.arange(NCL, dtype=jnp.int32)
    source = jnp.clip(cluster_ladder - (cluster_ladder > largest).astype(jnp.int32), 0, others - 1)
    cluster_sizes = jnp.where(cluster_ladder == largest, NEEDB, counts[source]).astype(jnp.int32)
    offsets = jnp.cumsum(cluster_sizes) - cluster_sizes
    pair_keys = jax.random.split(streams[3], NCL)
    pair_orders = jax.vmap(lambda one_key: jax.random.permutation(one_key, OV * OV))(pair_keys).astype(jnp.int32)
    position = jnp.arange(KEPT, dtype=jnp.int32)
    cluster_of = jnp.sum((position[:, None] >= offsets[None, :]).astype(jnp.int32), axis=1) - 1
    within = position - offsets[cluster_of]
    pair_code = pair_orders[cluster_of, within]
    row_block = cluster_blocks[cluster_of, pair_code // OV]
    col_block = cluster_blocks[cluster_of, pair_code % OV]
    holder_order = jax.random.permutation(streams[4], holders).astype(jnp.int32)
    holder = holder_order[position // 2 % holders]
    local_place = 2 * (position // (2 * holders)) + position % 2
    slot_index = holder * KT_DEV + local_place
    shuffle = jax.random.permutation(streams[5], KEPT).astype(jnp.int32)
    kept_tiles = jnp.zeros((KEPT, 2), jnp.int32).at[shuffle].set(jnp.stack([row_block, col_block], axis=1))
    tile_slot = jnp.zeros((KEPT,), jnp.int32).at[shuffle].set(slot_index)
    batch_slot = jax.random.permutation(streams[6], NBAT).astype(jnp.int32)
    batch_cluster = batch_slot // (BAT_DEV * DEV_CL)
    list_keys = jax.random.split(streams[7], NBAT)
    list_orders = jax.vmap(lambda one_key: jax.random.permutation(one_key, OV))(list_keys).astype(jnp.int32)
    blocks = jnp.take_along_axis(cluster_blocks[batch_cluster], list_orders, axis=1)
    return (kept_tiles, tile_slot, blocks, batch_slot)


def draw_kept_tiles(key, part):
    return layout(key)[0]


def draw_tile_slot(key, part):
    return layout(key)[1]


def draw_blocks(key, part):
    return layout(key)[2]


def draw_batch_slot(key, part):
    return layout(key)[3]


def levels(own_key, shape, cuts, least, high):
    loudness = 1.0
    for axis_at, shards_of in cuts:
        draws = jax.random.uniform(jax.random.fold_in(jax.random.fold_in(own_key, 6), axis_at), (shards_of,), jnp.float32, least / len(cuts), high / len(cuts))
        loudness = loudness * jnp.repeat(jnp.exp(draws), shape[axis_at] // shards_of).reshape((-1,) + (1,) * (len(shape) - 1 - axis_at))
    return loudness


def noise(rng, dims, scale, limit, cuts=(), kind=jnp.bfloat16):
    result = jax.random.normal(rng, dims, jnp.float32) * scale
    if len(cuts) > 0:
        result = levels(rng, dims, cuts, -0.22, 0.18) * result
    return jnp.clip(result, min=-limit, max=limit).astype(kind)


def setup_inputs(seed: int = 0, part: int = 0) -> dict:
    key_of = jax.random.split(jax.random.key(seed), 10)
    part_keys = jax.random.split(jax.random.fold_in(key_of[9], part), 10)
    return {
        "coeffs": noise(part_keys[0], (NS, NB), NS ** -0.5, 0.09375, ((0, 16),), jnp.float32),
        "occupation": jnp.clip(jax.random.uniform(part_keys[1], (NS,), jnp.float32, -1.0, 1.0) * levels(part_keys[1], (NS,), ((0, 16),), -0.4, 0.0), -1.0, 1.0),
        "kept_tiles": draw_kept_tiles(jax.random.fold_in(jax.random.fold_in(key_of[9], part), 71), part),
        "tile_slot": draw_tile_slot(jax.random.fold_in(jax.random.fold_in(key_of[9], part), 71), part),
        "blocks": draw_blocks(jax.random.fold_in(jax.random.fold_in(key_of[9], part), 71), part),
        "batch_slot": draw_batch_slot(jax.random.fold_in(jax.random.fold_in(key_of[9], part), 71), part),
        "tables": noise(part_keys[6], (NBAT, OV * BS, PTS), 0.6, 3.6, ((0, 16),), jnp.float32),
        "weights": jnp.clip(jnp.exp(math.log(0.05) - 2.3025851 * jax.random.uniform(part_keys[7], (NBAT, PTS), jnp.float32) ** levels(part_keys[7], (NBAT, PTS), ((0, 16),), -0.2, 0.2)), 0.005, 0.05),
        "local_pot": noise(part_keys[8], (NBAT, PTS), 1.0, 6.0, ((0, 16),), jnp.float32),
    }


def tile_products(coeffs, occupation, kept_tiles):
    blocked = coeffs.reshape(NS, NB // BS, BS)
    scaled = blocked * occupation[:, None, None]

    def one_tile(tile_pair):
        return jnp.einsum("sx,sy->xy", blocked[:, tile_pair[0], :], scaled[:, tile_pair[1], :], precision=lax.Precision.HIGHEST).reshape(BS * BS)

    return lax.map(one_tile, kept_tiles)


def tile_places(kept_tiles, block_lists):
    ladder = jnp.arange(block_lists.shape[-1], dtype=jnp.int32)
    row_match = kept_tiles[None, :, 0:1] == block_lists[:, None, :]
    col_match = kept_tiles[None, :, 1:2] == block_lists[:, None, :]
    present = jnp.any(row_match, axis=2) & jnp.any(col_match, axis=2)
    row_place = jnp.sum(jnp.where(row_match, ladder, 0), axis=2).astype(jnp.int32)
    col_place = jnp.sum(jnp.where(col_match, ladder, 0), axis=2).astype(jnp.int32)
    return present, row_place, col_place


def reference(coeffs, occupation, kept_tiles, tile_slot, blocks, batch_slot, tables, weights, local_pot):
    products = tile_products(coeffs, occupation, kept_tiles)
    slot_batch = jnp.zeros((NBAT,), jnp.int32).at[batch_slot].set(jnp.arange(NBAT, dtype=jnp.int32))
    slot_blocks = blocks[slot_batch]

    def per_batch(summed, inputs):
        table_rows, weight_row, base_row, block_list = inputs
        present, row_place, col_place = tile_places(kept_tiles, block_list[None, :])
        present = present[0]
        row_index = row_place[0]
        col_index = col_place[0]
        kept_values = jnp.where(present[:, None], products, 0.0).reshape(KEPT, BS, BS)
        dense_tiles = jnp.zeros((OV, BS, OV, BS), jnp.float32).at[row_index, :, col_index, :].add(kept_values)
        basis_grid = table_rows.reshape(OV, BS, PTS)
        mixed_rows = jnp.einsum("ixjy,jyp->ixp", dense_tiles, basis_grid, precision=lax.Precision.HIGHEST)
        density = jnp.sum(basis_grid * mixed_rows, axis=(0, 1))
        potential = base_row + density - density * density * density / 6.0
        weighted = basis_grid * (weight_row * potential)[None, None, :]
        full_matrix = jnp.einsum("ixp,jyp->ixjy", weighted, basis_grid, precision=lax.Precision.HIGHEST)
        picked = full_matrix[row_index, :, col_index, :].reshape(KEPT, BS * BS)
        return summed + jnp.where(present[:, None], picked, 0.0), density

    summed, density = lax.scan(per_batch, jnp.zeros((KEPT, BS * BS), jnp.float32), (tables, weights, local_pot, slot_blocks))
    matrix = jnp.zeros_like(summed).at[tile_slot].set(summed)
    return density, matrix
```

```python
import jax
import jax.numpy as jnp
from jax import lax
from jax.sharding import PartitionSpec as P

BS = 64
OV = 8


def body(coeffs, occupation, kept_tiles, tile_slot, blocks, batch_slot, tables, weights, local_pot):
    devices = lax.axis_size("tiles")
    my_index = lax.axis_index("tiles")
    kept_count = kept_tiles.shape[0]
    batch_count = tables.shape[0]
    batch_total = batch_slot.shape[0]
    state_count = coeffs.shape[0]
    block_total = coeffs.shape[1] // BS
    points = tables.shape[-1]
    width = OV * BS

    blocked = coeffs.reshape(state_count, block_total, BS)
    left_rows = jnp.take(blocked, kept_tiles[:, 0], axis=1)
    right_rows = jnp.take(blocked, kept_tiles[:, 1], axis=1) * occupation[:, None, None]
    partial = jnp.einsum(
        "srx,sry->rxy", left_rows, right_rows, precision=lax.Precision.HIGHEST
    ).reshape(kept_count, BS * BS)
    tile_values = lax.psum(partial, "tiles")

    ladder_batch = jnp.arange(batch_total, dtype=jnp.int32)
    slot_batch = jnp.zeros((batch_total,), jnp.int32).at[batch_slot].set(ladder_batch)
    my_batches = lax.dynamic_slice_in_dim(slot_batch, my_index * batch_count, batch_count)
    my_blocks = blocks[my_batches]
    canon = jnp.sort(my_blocks[0])
    ladder_ov = jnp.arange(OV, dtype=jnp.int32)
    match = my_blocks[:, :, None] == canon[None, None, :]
    source = jnp.sum(jnp.where(match, ladder_ov[None, :, None], 0), axis=1)
    grid = tables.reshape(batch_count, OV, BS, points)
    canon_tables = jnp.take_along_axis(grid, source[:, :, None, None], axis=1).reshape(
        batch_count, width, points
    )

    row_hit = kept_tiles[:, 0:1] == canon[None, :]
    col_hit = kept_tiles[:, 1:2] == canon[None, :]
    present = jnp.any(row_hit, axis=1) & jnp.any(col_hit, axis=1)
    row_place = jnp.sum(jnp.where(row_hit, ladder_ov[None, :], 0), axis=1)
    col_place = jnp.sum(jnp.where(col_hit, ladder_ov[None, :], 0), axis=1)
    kept_values = jnp.where(present[:, None], tile_values, 0.0).reshape(kept_count, BS, BS)
    dense = (
        jnp.zeros((OV, BS, OV, BS), jnp.float32)
        .at[row_place, :, col_place, :]
        .add(kept_values)
        .reshape(width, width)
    )
    mixed = jnp.einsum("uv,bvp->bup", dense, canon_tables, precision=lax.Precision.HIGH)
    density = jnp.sum(canon_tables * mixed, axis=1)
    potential = local_pot + density - density * density * density / 6.0
    weighted = canon_tables * (weights * potential)[:, None, :]
    full_matrix = jnp.einsum(
        "bup,bvp->uv", weighted, canon_tables, precision=lax.Precision.HIGH
    ).reshape(OV, BS, OV, BS)
    picked = full_matrix[row_place, :, col_place, :].reshape(kept_count, BS * BS)
    contrib = jnp.where(present[:, None], picked, 0.0)

    ladder_kept = jnp.arange(kept_count, dtype=jnp.int32)
    slot_kept = jnp.zeros((kept_count,), jnp.int32).at[tile_slot].set(ladder_kept)
    by_slot = contrib[slot_kept]
    matrix = lax.psum_scatter(by_slot, "tiles", scatter_dimension=0, tiled=True)
    return (density, matrix)


def solution(mesh):
    in_specs = (
        P(("groups", "tiles"), None),
        P(("groups", "tiles")),
        P("groups", None),
        P("groups"),
        P("groups", None),
        P("groups"),
        P(("groups", "tiles"), None, None),
        P(("groups", "tiles"), None),
        P(("groups", "tiles"), None),
    )
    out_specs = (P(("groups", "tiles"), None), P(("groups", "tiles"), None))
    return jax.shard_map(body, mesh=mesh, in_specs=in_specs, out_specs=out_specs, check_vma=False)
```

```python
import jax
import jax.numpy as jnp
from jax import lax
from jax.sharding import PartitionSpec as P

BS = 64
OV = 8


def body(coeffs, occupation, kept_tiles, tile_slot, blocks, batch_slot, tables, weights, local_pot):
    devices = lax.axis_size("tiles")
    my_index = lax.axis_index("tiles")
    kept_count = kept_tiles.shape[0]
    owned_count = kept_count // devices
    batch_count = tables.shape[0]
    batch_total = batch_slot.shape[0]
    state_count = coeffs.shape[0]
    block_total = coeffs.shape[1] // BS
    points = tables.shape[-1]
    width = OV * BS

    ladder_kept = jnp.arange(kept_count, dtype=jnp.int32)
    slot_kept = jnp.zeros((kept_count,), jnp.int32).at[tile_slot].set(ladder_kept)
    pairs = kept_tiles[slot_kept]
    wide = coeffs.reshape(state_count, block_total // 2, 2 * BS)

    def block_rows(block_ids):
        rows = jnp.take(wide, block_ids // 2, axis=1)
        return jnp.where((block_ids % 2 == 0)[None, :, None], rows[:, :, :BS], rows[:, :, BS:])

    left_rows = block_rows(pairs[:, 0])
    right_rows = block_rows(pairs[:, 1]) * occupation[:, None, None]
    partial = jnp.einsum(
        "srx,sry->rxy", left_rows, right_rows, precision=lax.Precision.HIGHEST
    ).reshape(devices, owned_count, BS * BS)
    owned = jnp.sum(lax.all_to_all(partial, "tiles", 0, 0, tiled=False), axis=0)
    spread = jnp.broadcast_to(owned[None], (devices, owned_count, BS * BS))
    tile_values = lax.all_to_all(spread, "tiles", 0, 0, tiled=False).reshape(kept_count, BS * BS)

    ladder_batch = jnp.arange(batch_total, dtype=jnp.int32)
    slot_batch = jnp.zeros((batch_total,), jnp.int32).at[batch_slot].set(ladder_batch)
    my_batches = lax.dynamic_slice_in_dim(slot_batch, my_index * batch_count, batch_count)
    my_blocks = blocks[my_batches]
    canon = jnp.sort(my_blocks[0])
    ladder_ov = jnp.arange(OV, dtype=jnp.int32)
    match = my_blocks[:, :, None] == canon[None, None, :]
    source = jnp.sum(jnp.where(match, ladder_ov[None, :, None], 0), axis=1)
    grid = tables.reshape(batch_count, OV, BS, points)
    canon_tables = jnp.take_along_axis(grid, source[:, :, None, None], axis=1).reshape(
        batch_count, width, points
    )

    row_hit = pairs[:, 0:1] == canon[None, :]
    col_hit = pairs[:, 1:2] == canon[None, :]
    present = jnp.any(row_hit, axis=1) & jnp.any(col_hit, axis=1)
    row_place = jnp.sum(jnp.where(row_hit, ladder_ov[None, :], 0), axis=1)
    col_place = jnp.sum(jnp.where(col_hit, ladder_ov[None, :], 0), axis=1)
    kept_values = jnp.where(present[:, None], tile_values, 0.0).reshape(kept_count, BS, BS)
    dense = (
        jnp.zeros((OV, BS, OV, BS), jnp.float32)
        .at[row_place, :, col_place, :]
        .add(kept_values)
        .reshape(width, width)
    )
    mixed = jnp.einsum("uv,bvp->bup", dense, canon_tables, precision=lax.Precision.HIGH)
    density = jnp.sum(canon_tables * mixed, axis=1)
    potential = local_pot + density - density * density * density / 6.0
    weighted = canon_tables * (weights * potential)[:, None, :]
    full_matrix = jnp.einsum(
        "bup,bvp->uv", weighted, canon_tables, precision=lax.Precision.HIGH
    ).reshape(OV, BS, OV, BS)
    picked = full_matrix[row_place, :, col_place, :].reshape(kept_count, BS * BS)
    contrib = jnp.where(present[:, None], picked, 0.0)

    terms = contrib.reshape(devices, owned_count, BS * BS)
    matrix = jnp.sum(lax.all_to_all(terms, "tiles", 0, 0, tiled=False), axis=0)
    return (density, matrix)


def solution(mesh):
    in_specs = (
        P(("groups", "tiles"), None),
        P(("groups", "tiles")),
        P("groups", None),
        P("groups"),
        P("groups", None),
        P("groups"),
        P(("groups", "tiles"), None, None),
        P(("groups", "tiles"), None),
        P(("groups", "tiles"), None),
    )
    out_specs = (P(("groups", "tiles"), None), P(("groups", "tiles"), None))
    return jax.shard_map(body, mesh=mesh, in_specs=in_specs, out_specs=out_specs, check_vma=False)
```

```python
import jax
import jax.numpy as jnp
from jax import lax
from jax.experimental import pallas as pl
from jax.experimental.pallas import tpu as pltpu
from jax.sharding import PartitionSpec as P

BS = 64
OV = 8


def tile_kernel(pairs_ref, left_ref, right_ref, occ_ref, out_ref):
    k = pl.program_id(0)
    row_block = pairs_ref[2 * k]
    col_block = pairs_ref[2 * k + 1]
    left = left_ref[...]
    right = right_ref[...] * occ_ref[...]
    left = jnp.where(row_block % 2 == 0, left[:, :BS], left[:, BS:])
    right = jnp.where(col_block % 2 == 0, right[:, :BS], right[:, BS:])
    out_ref[0] = lax.dot_general(
        left,
        right,
        (((0,), (0,)), ((), ())),
        precision=lax.Precision.HIGHEST,
        preferred_element_type=jnp.float32,
    )


def tile_products(coeffs, occupation, pairs):
    state_count = coeffs.shape[0]
    kept_count = pairs.shape[0]
    grid_spec = pltpu.PrefetchScalarGridSpec(
        num_scalar_prefetch=1,
        grid=(kept_count,),
        in_specs=[
            pl.BlockSpec((state_count, 2 * BS), lambda k, p: (0, p[2 * k] // 2)),
            pl.BlockSpec((state_count, 2 * BS), lambda k, p: (0, p[2 * k + 1] // 2)),
            pl.BlockSpec((state_count, 1), lambda k, p: (0, 0)),
        ],
        out_specs=pl.BlockSpec((1, BS, BS), lambda k, p: (k, 0, 0)),
    )
    return pl.pallas_call(
        tile_kernel,
        grid_spec=grid_spec,
        out_shape=jax.ShapeDtypeStruct((kept_count, BS, BS), jnp.float32),
    )(pairs.reshape(-1), coeffs, coeffs, occupation.reshape(state_count, 1))


def body(coeffs, occupation, kept_tiles, tile_slot, blocks, batch_slot, tables, weights, local_pot):
    devices = lax.axis_size("tiles")
    my_index = lax.axis_index("tiles")
    kept_count = kept_tiles.shape[0]
    owned_count = kept_count // devices
    batch_count = tables.shape[0]
    batch_total = batch_slot.shape[0]
    state_count = coeffs.shape[0]
    block_total = coeffs.shape[1] // BS
    points = tables.shape[-1]
    width = OV * BS

    ladder_kept = jnp.arange(kept_count, dtype=jnp.int32)
    slot_kept = jnp.zeros((kept_count,), jnp.int32).at[tile_slot].set(ladder_kept)
    pairs = kept_tiles[slot_kept]
    partial = tile_products(coeffs, occupation, pairs).reshape(devices, owned_count, BS * BS)
    owned = jnp.sum(lax.all_to_all(partial, "tiles", 0, 0, tiled=False), axis=0)
    spread = jnp.broadcast_to(owned[None], (devices, owned_count, BS * BS))
    tile_values = lax.all_to_all(spread, "tiles", 0, 0, tiled=False).reshape(kept_count, BS * BS)

    ladder_batch = jnp.arange(batch_total, dtype=jnp.int32)
    slot_batch = jnp.zeros((batch_total,), jnp.int32).at[batch_slot].set(ladder_batch)
    my_batches = lax.dynamic_slice_in_dim(slot_batch, my_index * batch_count, batch_count)
    my_blocks = blocks[my_batches]
    canon = jnp.sort(my_blocks[0])
    ladder_ov = jnp.arange(OV, dtype=jnp.int32)
    match = my_blocks[:, :, None] == canon[None, None, :]
    source = jnp.sum(jnp.where(match, ladder_ov[None, :, None], 0), axis=1)
    grid = tables.reshape(batch_count, OV, BS, points)
    canon_tables = jnp.take_along_axis(grid, source[:, :, None, None], axis=1).reshape(
        batch_count, width, points
    )

    row_hit = pairs[:, 0:1] == canon[None, :]
    col_hit = pairs[:, 1:2] == canon[None, :]
    present = jnp.any(row_hit, axis=1) & jnp.any(col_hit, axis=1)
    row_place = jnp.sum(jnp.where(row_hit, ladder_ov[None, :], 0), axis=1)
    col_place = jnp.sum(jnp.where(col_hit, ladder_ov[None, :], 0), axis=1)
    kept_values = jnp.where(present[:, None], tile_values, 0.0).reshape(kept_count, BS, BS)
    dense = (
        jnp.zeros((OV, BS, OV, BS), jnp.float32)
        .at[row_place, :, col_place, :]
        .add(kept_values)
        .reshape(width, width)
    )
    mixed = jnp.einsum("uv,bvp->bup", dense, canon_tables, precision=lax.Precision.HIGH)
    density = jnp.sum(canon_tables * mixed, axis=1)
    potential = local_pot + density - density * density * density / 6.0
    weighted = canon_tables * (weights * potential)[:, None, :]
    full_matrix = jnp.einsum(
        "bup,bvp->uv", weighted, canon_tables, precision=lax.Precision.HIGH
    ).reshape(OV, BS, OV, BS)
    picked = full_matrix[row_place, :, col_place, :].reshape(kept_count, BS * BS)
    contrib = jnp.where(present[:, None], picked, 0.0)

    terms = contrib.reshape(devices, owned_count, BS * BS)
    matrix = jnp.sum(lax.all_to_all(terms, "tiles", 0, 0, tiled=False), axis=0)
    return (density, matrix)


def solution(mesh):
    in_specs = (
        P(("groups", "tiles"), None),
        P(("groups", "tiles")),
        P("groups", None),
        P("groups"),
        P("groups", None),
        P("groups"),
        P(("groups", "tiles"), None, None),
        P(("groups", "tiles"), None),
        P(("groups", "tiles"), None),
    )
    out_specs = (P(("groups", "tiles"), None), P(("groups", "tiles"), None))
    return jax.shard_map(body, mesh=mesh, in_specs=in_specs, out_specs=out_specs, check_vma=False)
```

```python
import jax
import jax.numpy as jnp
from jax import lax
from jax.experimental import pallas as pl
from jax.experimental.pallas import tpu as pltpu
from jax.sharding import PartitionSpec as P

BS = 64
OV = 8


def tile_kernel(pairs_ref, left_ref, right_ref, occ_ref, out_ref):
    k = pl.program_id(0)
    row_block = pairs_ref[2 * k]
    col_block = pairs_ref[2 * k + 1]
    left = left_ref[...]
    right = right_ref[...] * occ_ref[...]
    left = jnp.where(row_block % 2 == 0, left[:, :BS], left[:, BS:])
    right = jnp.where(col_block % 2 == 0, right[:, :BS], right[:, BS:])
    out_ref[0] = lax.dot_general(
        left,
        right,
        (((0,), (0,)), ((), ())),
        precision=lax.Precision.HIGHEST,
        preferred_element_type=jnp.float32,
    )


def tile_products(coeffs, occupation, pairs):
    state_count = coeffs.shape[0]
    kept_count = pairs.shape[0]
    grid_spec = pltpu.PrefetchScalarGridSpec(
        num_scalar_prefetch=1,
        grid=(kept_count,),
        in_specs=[
            pl.BlockSpec((state_count, 2 * BS), lambda k, p: (0, p[2 * k] // 2)),
            pl.BlockSpec((state_count, 2 * BS), lambda k, p: (0, p[2 * k + 1] // 2)),
            pl.BlockSpec((state_count, 1), lambda k, p: (0, 0)),
        ],
        out_specs=pl.BlockSpec((1, BS, BS), lambda k, p: (k, 0, 0)),
    )
    return pl.pallas_call(
        tile_kernel,
        grid_spec=grid_spec,
        out_shape=jax.ShapeDtypeStruct((kept_count, BS, BS), jnp.float32),
    )(pairs.reshape(-1), coeffs, coeffs, occupation.reshape(state_count, 1))


def split_dot(left, right, dims):
    left_hi = left.astype(jnp.bfloat16)
    left_lo = (left - left_hi.astype(jnp.float32)).astype(jnp.bfloat16)
    right_hi = right.astype(jnp.bfloat16)
    right_lo = (right - right_hi.astype(jnp.float32)).astype(jnp.bfloat16)

    def one(a, b):
        return lax.dot_general(a, b, (dims, ((), ())), preferred_element_type=jnp.float32)

    return one(left_hi, right_hi) + (one(left_hi, right_lo) + one(left_lo, right_hi))


def batch_kernel(source_ref, table_ref, dense_ref, weight_ref, base_ref, density_ref, matrix_ref, canon_ref):
    b = pl.program_id(0)
    for q in range(OV):
        start = pl.multiple_of(source_ref[b * OV + q] * BS, BS)
        canon_ref[q * BS:(q + 1) * BS, :] = table_ref[0, pl.ds(start, BS), :]
    grid = canon_ref[...]
    mixed = split_dot(dense_ref[...], grid, ((1,), (0,)))
    density = jnp.sum(grid * mixed, axis=0, keepdims=True)
    potential = base_ref[0] + density - density * density * density / 6.0
    density_ref[0] = density
    weighted = grid * (weight_ref[0] * potential)
    terms = split_dot(weighted, grid, ((1,), (1,)))

    @pl.when(b == 0)
    def _():
        matrix_ref[...] = terms

    @pl.when(b > 0)
    def _():
        matrix_ref[...] += terms


def batch_terms(source, tables, dense, weights, local_pot):
    batch_count, rows, points = tables.shape
    grid_spec = pltpu.PrefetchScalarGridSpec(
        num_scalar_prefetch=1,
        grid=(batch_count,),
        in_specs=[
            pl.BlockSpec((1, rows, points), lambda b, s: (b, 0, 0)),
            pl.BlockSpec((rows, rows), lambda b, s: (0, 0)),
            pl.BlockSpec((1, 1, points), lambda b, s: (b, 0, 0)),
            pl.BlockSpec((1, 1, points), lambda b, s: (b, 0, 0)),
        ],
        out_specs=[
            pl.BlockSpec((1, 1, points), lambda b, s: (b, 0, 0)),
            pl.BlockSpec((rows, rows), lambda b, s: (0, 0)),
        ],
        scratch_shapes=[pltpu.VMEM((rows, points), jnp.float32)],
    )
    density, matrix = pl.pallas_call(
        batch_kernel,
        grid_spec=grid_spec,
        out_shape=[
            jax.ShapeDtypeStruct((batch_count, 1, points), jnp.float32),
            jax.ShapeDtypeStruct((rows, rows), jnp.float32),
        ],
    )(
        source.reshape(-1),
        tables,
        dense,
        weights.reshape(batch_count, 1, points),
        local_pot.reshape(batch_count, 1, points),
    )
    return density.reshape(batch_count, points), matrix


def body(coeffs, occupation, kept_tiles, tile_slot, blocks, batch_slot, tables, weights, local_pot):
    devices = lax.axis_size("tiles")
    my_index = lax.axis_index("tiles")
    kept_count = kept_tiles.shape[0]
    owned_count = kept_count // devices
    batch_count = tables.shape[0]
    batch_total = batch_slot.shape[0]
    state_count = coeffs.shape[0]
    block_total = coeffs.shape[1] // BS
    points = tables.shape[-1]
    width = OV * BS

    ladder_kept = jnp.arange(kept_count, dtype=jnp.int32)
    slot_kept = jnp.zeros((kept_count,), jnp.int32).at[tile_slot].set(ladder_kept)
    pairs = kept_tiles[slot_kept]
    partial = tile_products(coeffs, occupation, pairs).reshape(devices, owned_count, BS * BS)
    owned = jnp.sum(lax.all_to_all(partial, "tiles", 0, 0, tiled=False), axis=0)
    spread = jnp.broadcast_to(owned[None], (devices, owned_count, BS * BS))
    tile_values = lax.all_to_all(spread, "tiles", 0, 0, tiled=False).reshape(kept_count, BS * BS)

    ladder_batch = jnp.arange(batch_total, dtype=jnp.int32)
    slot_batch = jnp.zeros((batch_total,), jnp.int32).at[batch_slot].set(ladder_batch)
    my_batches = lax.dynamic_slice_in_dim(slot_batch, my_index * batch_count, batch_count)
    my_blocks = blocks[my_batches]
    canon = jnp.sort(my_blocks[0])
    ladder_ov = jnp.arange(OV, dtype=jnp.int32)
    match = my_blocks[:, :, None] == canon[None, None, :]
    source = jnp.sum(jnp.where(match, ladder_ov[None, :, None], 0), axis=1)
    row_hit = pairs[:, 0:1] == canon[None, :]
    col_hit = pairs[:, 1:2] == canon[None, :]
    present = jnp.any(row_hit, axis=1) & jnp.any(col_hit, axis=1)
    row_place = jnp.sum(jnp.where(row_hit, ladder_ov[None, :], 0), axis=1)
    col_place = jnp.sum(jnp.where(col_hit, ladder_ov[None, :], 0), axis=1)
    kept_values = jnp.where(present[:, None], tile_values, 0.0).reshape(kept_count, BS, BS)
    dense = (
        jnp.zeros((OV, BS, OV, BS), jnp.float32)
        .at[row_place, :, col_place, :]
        .add(kept_values)
        .reshape(width, width)
    )
    density, full_matrix = batch_terms(source, tables, dense, weights, local_pot)
    full_matrix = full_matrix.reshape(OV, BS, OV, BS)
    picked = full_matrix[row_place, :, col_place, :].reshape(kept_count, BS * BS)
    contrib = jnp.where(present[:, None], picked, 0.0)

    terms = contrib.reshape(devices, owned_count, BS * BS)
    matrix = jnp.sum(lax.all_to_all(terms, "tiles", 0, 0, tiled=False), axis=0)
    return (density, matrix)


def solution(mesh):
    in_specs = (
        P(("groups", "tiles"), None),
        P(("groups", "tiles")),
        P("groups", None),
        P("groups"),
        P("groups", None),
        P("groups"),
        P(("groups", "tiles"), None, None),
        P(("groups", "tiles"), None),
        P(("groups", "tiles"), None),
    )
    out_specs = (P(("groups", "tiles"), None), P(("groups", "tiles"), None))
    return jax.shard_map(body, mesh=mesh, in_specs=in_specs, out_specs=out_specs, check_vma=False)
```

```python
import jax
import jax.numpy as jnp
from jax import lax
from jax.experimental import pallas as pl
from jax.experimental.pallas import tpu as pltpu
from jax.sharding import PartitionSpec as P

BS = 64
OV = 8


def tile_kernel(pairs_ref, *refs):
    group = (len(refs) - 2) // 2
    occ_ref = refs[2 * group]
    out_ref = refs[2 * group + 1]
    k = pl.program_id(0)
    occ = occ_ref[...]
    for i in range(group):
        row_block = pairs_ref[2 * (group * k + i)]
        col_block = pairs_ref[2 * (group * k + i) + 1]
        left = refs[i][...]
        right = refs[group + i][...] * occ
        left = jnp.where(row_block % 2 == 0, left[:, :BS], left[:, BS:])
        right = jnp.where(col_block % 2 == 0, right[:, :BS], right[:, BS:])
        out_ref[i] = lax.dot_general(
            left,
            right,
            (((0,), (0,)), ((), ())),
            precision=lax.Precision.HIGHEST,
            preferred_element_type=jnp.float32,
        )


def tile_products(coeffs, occupation, pairs):
    state_count = coeffs.shape[0]
    kept_count = pairs.shape[0]
    group = next(g for g in (4, 2, 1) if kept_count % g == 0)

    def block_of(i, side):
        return pl.BlockSpec(
            (state_count, 2 * BS), lambda k, p: (0, p[2 * (group * k + i) + side] // 2)
        )

    grid_spec = pltpu.PrefetchScalarGridSpec(
        num_scalar_prefetch=1,
        grid=(kept_count // group,),
        in_specs=[block_of(i, 0) for i in range(group)]
        + [block_of(i, 1) for i in range(group)]
        + [pl.BlockSpec((state_count, 1), lambda k, p: (0, 0))],
        out_specs=pl.BlockSpec((group, BS, BS), lambda k, p: (k, 0, 0)),
    )
    return pl.pallas_call(
        tile_kernel,
        grid_spec=grid_spec,
        out_shape=jax.ShapeDtypeStruct((kept_count, BS, BS), jnp.float32),
    )(pairs.reshape(-1), *([coeffs] * (2 * group)), occupation.reshape(state_count, 1))


def split_dot(left, right, dims):
    left_hi = left.astype(jnp.bfloat16)
    left_lo = (left - left_hi.astype(jnp.float32)).astype(jnp.bfloat16)
    right_hi = right.astype(jnp.bfloat16)
    right_lo = (right - right_hi.astype(jnp.float32)).astype(jnp.bfloat16)

    def one(a, b):
        return lax.dot_general(a, b, (dims, ((), ())), preferred_element_type=jnp.float32)

    return one(left_hi, right_hi) + (one(left_hi, right_lo) + one(left_lo, right_hi))


def batch_kernel(source_ref, table_ref, dense_ref, weight_ref, base_ref, density_ref, matrix_ref, canon_ref):
    b = pl.program_id(0)
    for q in range(OV):
        start = pl.multiple_of(source_ref[b * OV + q] * BS, BS)
        canon_ref[q * BS:(q + 1) * BS, :] = table_ref[0, pl.ds(start, BS), :]
    grid = canon_ref[...]
    mixed = split_dot(dense_ref[...], grid, ((1,), (0,)))
    density = jnp.sum(grid * mixed, axis=0, keepdims=True)
    potential = base_ref[0] + density - density * density * density / 6.0
    density_ref[0] = density
    weighted = grid * (weight_ref[0] * potential)
    terms = split_dot(weighted, grid, ((1,), (1,)))

    @pl.when(b == 0)
    def _():
        matrix_ref[...] = terms

    @pl.when(b > 0)
    def _():
        matrix_ref[...] += terms


def batch_terms(source, tables, dense, weights, local_pot):
    batch_count, rows, points = tables.shape
    grid_spec = pltpu.PrefetchScalarGridSpec(
        num_scalar_prefetch=1,
        grid=(batch_count,),
        in_specs=[
            pl.BlockSpec((1, rows, points), lambda b, s: (b, 0, 0)),
            pl.BlockSpec((rows, rows), lambda b, s: (0, 0)),
            pl.BlockSpec((1, 1, points), lambda b, s: (b, 0, 0)),
            pl.BlockSpec((1, 1, points), lambda b, s: (b, 0, 0)),
        ],
        out_specs=[
            pl.BlockSpec((1, 1, points), lambda b, s: (b, 0, 0)),
            pl.BlockSpec((rows, rows), lambda b, s: (0, 0)),
        ],
        scratch_shapes=[pltpu.VMEM((rows, points), jnp.float32)],
    )
    density, matrix = pl.pallas_call(
        batch_kernel,
        grid_spec=grid_spec,
        out_shape=[
            jax.ShapeDtypeStruct((batch_count, 1, points), jnp.float32),
            jax.ShapeDtypeStruct((rows, rows), jnp.float32),
        ],
    )(
        source.reshape(-1),
        tables,
        dense,
        weights.reshape(batch_count, 1, points),
        local_pot.reshape(batch_count, 1, points),
    )
    return density.reshape(batch_count, points), matrix


def body(coeffs, occupation, kept_tiles, tile_slot, blocks, batch_slot, tables, weights, local_pot):
    devices = lax.axis_size("tiles")
    my_index = lax.axis_index("tiles")
    kept_count = kept_tiles.shape[0]
    owned_count = kept_count // devices
    batch_count = tables.shape[0]
    batch_total = batch_slot.shape[0]
    state_count = coeffs.shape[0]
    block_total = coeffs.shape[1] // BS
    points = tables.shape[-1]
    width = OV * BS

    ladder_kept = jnp.arange(kept_count, dtype=jnp.int32)
    slot_kept = jnp.zeros((kept_count,), jnp.int32).at[tile_slot].set(ladder_kept)
    pairs = kept_tiles[slot_kept]
    partial = tile_products(coeffs, occupation, pairs).reshape(devices, owned_count, BS * BS)
    owned = jnp.sum(lax.all_to_all(partial, "tiles", 0, 0, tiled=False), axis=0)
    spread = jnp.broadcast_to(owned[None], (devices, owned_count, BS * BS))
    tile_values = lax.all_to_all(spread, "tiles", 0, 0, tiled=False).reshape(kept_count, BS * BS)

    ladder_batch = jnp.arange(batch_total, dtype=jnp.int32)
    slot_batch = jnp.zeros((batch_total,), jnp.int32).at[batch_slot].set(ladder_batch)
    my_batches = lax.dynamic_slice_in_dim(slot_batch, my_index * batch_count, batch_count)
    my_blocks = blocks[my_batches]
    canon = jnp.sort(my_blocks[0])
    ladder_ov = jnp.arange(OV, dtype=jnp.int32)
    match = my_blocks[:, :, None] == canon[None, None, :]
    source = jnp.sum(jnp.where(match, ladder_ov[None, :, None], 0), axis=1)
    row_hit = pairs[:, 0:1] == canon[None, :]
    col_hit = pairs[:, 1:2] == canon[None, :]
    present = jnp.any(row_hit, axis=1) & jnp.any(col_hit, axis=1)
    row_place = jnp.sum(jnp.where(row_hit, ladder_ov[None, :], 0), axis=1)
    col_place = jnp.sum(jnp.where(col_hit, ladder_ov[None, :], 0), axis=1)
    kept_values = jnp.where(present[:, None], tile_values, 0.0).reshape(kept_count, BS, BS)
    dense = (
        jnp.zeros((OV, BS, OV, BS), jnp.float32)
        .at[row_place, :, col_place, :]
        .add(kept_values)
        .reshape(width, width)
    )
    density, full_matrix = batch_terms(source, tables, dense, weights, local_pot)
    full_matrix = full_matrix.reshape(OV, BS, OV, BS)
    picked = full_matrix[row_place, :, col_place, :].reshape(kept_count, BS * BS)
    contrib = jnp.where(present[:, None], picked, 0.0)

    terms = contrib.reshape(devices, owned_count, BS * BS)
    matrix = jnp.sum(lax.all_to_all(terms, "tiles", 0, 0, tiled=False), axis=0)
    return (density, matrix)


def solution(mesh):
    in_specs = (
        P(("groups", "tiles"), None),
        P(("groups", "tiles")),
        P("groups", None),
        P("groups"),
        P("groups", None),
        P("groups"),
        P(("groups", "tiles"), None, None),
        P(("groups", "tiles"), None),
        P(("groups", "tiles"), None),
    )
    out_specs = (P(("groups", "tiles"), None), P(("groups", "tiles"), None))
    return jax.shard_map(body, mesh=mesh, in_specs=in_specs, out_specs=out_specs, check_vma=False)
```

```python
import jax
import jax.numpy as jnp
from jax import lax
from jax.experimental import pallas as pl
from jax.experimental.pallas import tpu as pltpu
from jax.sharding import PartitionSpec as P

BS = 64
OV = 8


def tile_kernel(pairs_ref, *refs):
    group = (len(refs) - 2) // 2
    occ_ref = refs[2 * group]
    out_ref = refs[2 * group + 1]
    k = pl.program_id(0)
    occ = occ_ref[...]
    for i in range(group):
        row_block = pairs_ref[2 * (group * k + i)]
        col_block = pairs_ref[2 * (group * k + i) + 1]
        left = refs[i][...]
        right = refs[group + i][...] * occ
        left = jnp.where(row_block % 2 == 0, left[:, :BS], left[:, BS:])
        right = jnp.where(col_block % 2 == 0, right[:, :BS], right[:, BS:])
        out_ref[i] = lax.dot_general(
            left,
            right,
            (((0,), (0,)), ((), ())),
            precision=lax.Precision.HIGHEST,
            preferred_element_type=jnp.float32,
        )


def tile_products(coeffs, occupation, pairs):
    state_count = coeffs.shape[0]
    kept_count = pairs.shape[0]
    group = next(g for g in (8, 4, 2, 1) if kept_count % g == 0)

    def block_of(i, side):
        return pl.BlockSpec(
            (state_count, 2 * BS), lambda k, p: (0, p[2 * (group * k + i) + side] // 2)
        )

    grid_spec = pltpu.PrefetchScalarGridSpec(
        num_scalar_prefetch=1,
        grid=(kept_count // group,),
        in_specs=[block_of(i, 0) for i in range(group)]
        + [block_of(i, 1) for i in range(group)]
        + [pl.BlockSpec((state_count, 1), lambda k, p: (0, 0))],
        out_specs=pl.BlockSpec((group, BS, BS), lambda k, p: (k, 0, 0)),
    )
    return pl.pallas_call(
        tile_kernel,
        grid_spec=grid_spec,
        out_shape=jax.ShapeDtypeStruct((kept_count, BS, BS), jnp.float32),
    )(pairs.reshape(-1), *([coeffs] * (2 * group)), occupation.reshape(state_count, 1))


def split_dot(left, right, dims):
    left_hi = left.astype(jnp.bfloat16)
    left_lo = (left - left_hi.astype(jnp.float32)).astype(jnp.bfloat16)
    right_hi = right.astype(jnp.bfloat16)
    right_lo = (right - right_hi.astype(jnp.float32)).astype(jnp.bfloat16)

    def one(a, b):
        return lax.dot_general(a, b, (dims, ((), ())), preferred_element_type=jnp.float32)

    return one(left_hi, right_hi) + (one(left_hi, right_lo) + one(left_lo, right_hi))


def batch_kernel(
    source_ref, pick_ref, table_ref, tile_ref, weight_ref, base_ref,
    density_ref, pair_ref, canon_ref, dense_hi_ref, dense_lo_ref, acc_ref,
):
    b = pl.program_id(0)

    @pl.when(b == 0)
    def _():
        for q1 in range(OV):
            for q2 in range(OV):
                which = pick_ref[q1 * OV + q2]
                tile = jnp.where(which >= 0, tile_ref[jnp.maximum(which, 0)], 0.0)
                tile_hi = tile.astype(jnp.bfloat16)
                tile_lo = (tile - tile_hi.astype(jnp.float32)).astype(jnp.bfloat16)
                dense_hi_ref[q1 * BS:(q1 + 1) * BS, q2 * BS:(q2 + 1) * BS] = tile_hi
                dense_lo_ref[q1 * BS:(q1 + 1) * BS, q2 * BS:(q2 + 1) * BS] = tile_lo

    for q in range(OV):
        start = pl.multiple_of(source_ref[b * OV + q] * BS, BS)
        canon_ref[q * BS:(q + 1) * BS, :] = table_ref[0, pl.ds(start, BS), :]
    grid = canon_ref[...]
    grid_hi = grid.astype(jnp.bfloat16)
    grid_lo = (grid - grid_hi.astype(jnp.float32)).astype(jnp.bfloat16)

    def nn(a, c):
        return lax.dot_general(a, c, (((1,), (0,)), ((), ())), preferred_element_type=jnp.float32)

    dense_hi = dense_hi_ref[...]
    mixed = nn(dense_hi, grid_hi) + (nn(dense_hi, grid_lo) + nn(dense_lo_ref[...], grid_hi))
    density = jnp.sum(grid * mixed, axis=0, keepdims=True)
    potential = base_ref[0] + density - density * density * density / 6.0
    density_ref[0] = density
    weighted = grid * (weight_ref[0] * potential)
    terms = split_dot(weighted, grid, ((1,), (1,)))

    @pl.when(b == 0)
    def _():
        acc_ref[...] = terms

    @pl.when(b > 0)
    def _():
        acc_ref[...] += terms

    @pl.when(b == pl.num_programs(0) - 1)
    def _():
        for q1 in range(OV):
            for q2 in range(OV):
                pair_ref[q1 * OV + q2] = acc_ref[q1 * BS:(q1 + 1) * BS, q2 * BS:(q2 + 1) * BS]


def batch_terms(source, pick, tables, tile_values, weights, local_pot):
    batch_count, rows, points = tables.shape
    kept_count = tile_values.shape[0]
    grid_spec = pltpu.PrefetchScalarGridSpec(
        num_scalar_prefetch=2,
        grid=(batch_count,),
        in_specs=[
            pl.BlockSpec((1, rows, points), lambda b, s, k: (b, 0, 0)),
            pl.BlockSpec((kept_count, BS, BS), lambda b, s, k: (0, 0, 0)),
            pl.BlockSpec((1, 1, points), lambda b, s, k: (b, 0, 0)),
            pl.BlockSpec((1, 1, points), lambda b, s, k: (b, 0, 0)),
        ],
        out_specs=[
            pl.BlockSpec((1, 1, points), lambda b, s, k: (b, 0, 0)),
            pl.BlockSpec((OV * OV, BS, BS), lambda b, s, k: (0, 0, 0)),
        ],
        scratch_shapes=[
            pltpu.VMEM((rows, points), jnp.float32),
            pltpu.VMEM((rows, rows), jnp.bfloat16),
            pltpu.VMEM((rows, rows), jnp.bfloat16),
            pltpu.VMEM((rows, rows), jnp.float32),
        ],
    )
    density, pair_tiles = pl.pallas_call(
        batch_kernel,
        grid_spec=grid_spec,
        out_shape=[
            jax.ShapeDtypeStruct((batch_count, 1, points), jnp.float32),
            jax.ShapeDtypeStruct((OV * OV, BS, BS), jnp.float32),
        ],
    )(
        source.reshape(-1),
        pick,
        tables,
        tile_values,
        weights.reshape(batch_count, 1, points),
        local_pot.reshape(batch_count, 1, points),
    )
    return density.reshape(batch_count, points), pair_tiles


def body(coeffs, occupation, kept_tiles, tile_slot, blocks, batch_slot, tables, weights, local_pot):
    devices = lax.axis_size("tiles")
    my_index = lax.axis_index("tiles")
    kept_count = kept_tiles.shape[0]
    owned_count = kept_count // devices
    batch_count = tables.shape[0]
    batch_total = batch_slot.shape[0]
    state_count = coeffs.shape[0]
    block_total = coeffs.shape[1] // BS
    points = tables.shape[-1]
    width = OV * BS

    ladder_kept = jnp.arange(kept_count, dtype=jnp.int32)
    slot_kept = jnp.zeros((kept_count,), jnp.int32).at[tile_slot].set(ladder_kept)
    pairs = kept_tiles[slot_kept]
    partial = tile_products(coeffs, occupation, pairs).reshape(devices, owned_count, BS, BS)
    owned = jnp.sum(lax.all_to_all(partial, "tiles", 0, 0, tiled=False), axis=0)
    spread = jnp.broadcast_to(owned[None], (devices, owned_count, BS, BS))
    tile_values = lax.all_to_all(spread, "tiles", 0, 0, tiled=False).reshape(kept_count, BS, BS)

    ladder_batch = jnp.arange(batch_total, dtype=jnp.int32)
    slot_batch = jnp.zeros((batch_total,), jnp.int32).at[batch_slot].set(ladder_batch)
    my_batches = lax.dynamic_slice_in_dim(slot_batch, my_index * batch_count, batch_count)
    my_blocks = blocks[my_batches]
    canon = jnp.sort(my_blocks[0])
    ladder_ov = jnp.arange(OV, dtype=jnp.int32)
    match = my_blocks[:, :, None] == canon[None, None, :]
    source = jnp.sum(jnp.where(match, ladder_ov[None, :, None], 0), axis=1)
    row_hit = pairs[:, 0:1] == canon[None, :]
    col_hit = pairs[:, 1:2] == canon[None, :]
    present = jnp.any(row_hit, axis=1) & jnp.any(col_hit, axis=1)
    row_place = jnp.sum(jnp.where(row_hit, ladder_ov[None, :], 0), axis=1)
    col_place = jnp.sum(jnp.where(col_hit, ladder_ov[None, :], 0), axis=1)
    pair_code = row_place * OV + col_place
    ladder_pair = jnp.arange(OV * OV, dtype=jnp.int32)
    at_pair = present[None, :] & (pair_code[None, :] == ladder_pair[:, None])
    pick = jnp.where(
        jnp.any(at_pair, axis=1), jnp.sum(jnp.where(at_pair, ladder_kept[None, :], 0), axis=1), -1
    )
    density, pair_tiles = batch_terms(source, pick, tables, tile_values, weights, local_pot)
    contrib = jnp.where(present[:, None, None], pair_tiles[pair_code], 0.0)

    terms = contrib.reshape(devices, owned_count, BS, BS)
    matrix = jnp.sum(lax.all_to_all(terms, "tiles", 0, 0, tiled=False), axis=0)
    matrix = matrix.reshape(owned_count, BS * BS)
    return (density, matrix)


def solution(mesh):
    in_specs = (
        P(("groups", "tiles"), None),
        P(("groups", "tiles")),
        P("groups", None),
        P("groups"),
        P("groups", None),
        P("groups"),
        P(("groups", "tiles"), None, None),
        P(("groups", "tiles"), None),
        P(("groups", "tiles"), None),
    )
    out_specs = (P(("groups", "tiles"), None), P(("groups", "tiles"), None))
    return jax.shard_map(body, mesh=mesh, in_specs=in_specs, out_specs=out_specs, check_vma=False)
```

```python
import jax
import jax.numpy as jnp
from jax import lax
from jax.experimental import pallas as pl
from jax.experimental.pallas import tpu as pltpu
from jax.sharding import PartitionSpec as P

BS = 64
OV = 8


def tile_kernel(pairs_ref, *refs):
    group = (len(refs) - 2) // 2
    occ_ref = refs[2 * group]
    out_ref = refs[2 * group + 1]
    k = pl.program_id(0)
    occ = occ_ref[...]
    for i in range(group):
        row_block = pairs_ref[2 * (group * k + i)]
        col_block = pairs_ref[2 * (group * k + i) + 1]
        left = refs[i][...]
        right = refs[group + i][...] * occ
        left = jnp.where(row_block % 2 == 0, left[:, :BS], left[:, BS:])
        right = jnp.where(col_block % 2 == 0, right[:, :BS], right[:, BS:])
        out_ref[i] = lax.dot_general(
            left,
            right,
            (((0,), (0,)), ((), ())),
            precision=lax.Precision.HIGHEST,
            preferred_element_type=jnp.float32,
        )


def tile_products(coeffs, occupation, pairs):
    state_count = coeffs.shape[0]
    kept_count = pairs.shape[0]
    group = next(g for g in (8, 4, 2, 1) if kept_count % g == 0)

    def block_of(i, side):
        return pl.BlockSpec(
            (state_count, 2 * BS), lambda k, p: (0, p[2 * (group * k + i) + side] // 2)
        )

    grid_spec = pltpu.PrefetchScalarGridSpec(
        num_scalar_prefetch=1,
        grid=(kept_count // group,),
        in_specs=[block_of(i, 0) for i in range(group)]
        + [block_of(i, 1) for i in range(group)]
        + [pl.BlockSpec((state_count, 1), lambda k, p: (0, 0))],
        out_specs=pl.BlockSpec((group, BS, BS), lambda k, p: (k, 0, 0)),
    )
    return pl.pallas_call(
        tile_kernel,
        grid_spec=grid_spec,
        out_shape=jax.ShapeDtypeStruct((kept_count, BS, BS), jnp.float32),
    )(pairs.reshape(-1), *([coeffs] * (2 * group)), occupation.reshape(state_count, 1))


def split_dot(left, right, dims):
    left_hi = left.astype(jnp.bfloat16)
    left_lo = (left - left_hi.astype(jnp.float32)).astype(jnp.bfloat16)
    right_hi = right.astype(jnp.bfloat16)
    right_lo = (right - right_hi.astype(jnp.float32)).astype(jnp.bfloat16)

    def one(a, b):
        return lax.dot_general(a, b, (dims, ((), ())), preferred_element_type=jnp.float32)

    return one(left_hi, right_hi) + (one(left_hi, right_lo) + one(left_lo, right_hi))


def batch_kernel(
    source_ref, pick_ref, table_hbm, tile_hbm, weight_ref, base_ref,
    density_ref, pair_ref, canon_ref, stage_ref, dense_hi_ref, dense_lo_ref, table_sems, tile_sems,
):
    batch_count, _, points = table_hbm.shape
    copies = []
    for b in range(batch_count):
        for q in range(OV):
            start = pl.multiple_of(source_ref[b * OV + q] * BS, BS)
            copy = pltpu.make_async_copy(
                table_hbm.at[b, pl.ds(start, BS), :],
                canon_ref.at[q * BS:(q + 1) * BS, b * points:(b + 1) * points],
                table_sems.at[b * OV + q],
            )
            copy.start()
            copies.append(copy)
    for p in range(OV * OV):
        copy = pltpu.make_async_copy(
            tile_hbm.at[jnp.maximum(pick_ref[p], 0)], stage_ref.at[p], tile_sems.at[p]
        )
        copy.start()
        copies.append(copy)
    for copy in copies[batch_count * OV:]:
        copy.wait()
    for q1 in range(OV):
        for q2 in range(OV):
            p = q1 * OV + q2
            tile = jnp.where(pick_ref[p] >= 0, stage_ref[p], 0.0)
            tile_hi = tile.astype(jnp.bfloat16)
            tile_lo = (tile - tile_hi.astype(jnp.float32)).astype(jnp.bfloat16)
            dense_hi_ref[q1 * BS:(q1 + 1) * BS, q2 * BS:(q2 + 1) * BS] = tile_hi
            dense_lo_ref[q1 * BS:(q1 + 1) * BS, q2 * BS:(q2 + 1) * BS] = tile_lo
    for copy in copies[:batch_count * OV]:
        copy.wait()

    grid = canon_ref[...]
    grid_hi = grid.astype(jnp.bfloat16)
    grid_lo = (grid - grid_hi.astype(jnp.float32)).astype(jnp.bfloat16)

    def nn(a, c):
        return lax.dot_general(a, c, (((1,), (0,)), ((), ())), preferred_element_type=jnp.float32)

    dense_hi = dense_hi_ref[...]
    mixed = nn(dense_hi, grid_hi) + (nn(dense_hi, grid_lo) + nn(dense_lo_ref[...], grid_hi))
    density = jnp.sum(grid * mixed, axis=0, keepdims=True)
    potential = base_ref[...] + density - density * density * density / 6.0
    density_ref[...] = density
    weighted = grid * (weight_ref[...] * potential)
    terms = split_dot(weighted, grid, ((1,), (1,)))
    for q1 in range(OV):
        for q2 in range(OV):
            pair_ref[q1 * OV + q2] = terms[q1 * BS:(q1 + 1) * BS, q2 * BS:(q2 + 1) * BS]


def batch_terms(source, pick, tables, tile_values, weights, local_pot):
    batch_count, rows, points = tables.shape
    span = batch_count * points
    whole = lambda i, s, k: (0, 0)
    grid_spec = pltpu.PrefetchScalarGridSpec(
        num_scalar_prefetch=2,
        grid=(1,),
        in_specs=[
            pl.BlockSpec(memory_space=pl.ANY),
            pl.BlockSpec(memory_space=pl.ANY),
            pl.BlockSpec((1, span), whole),
            pl.BlockSpec((1, span), whole),
        ],
        out_specs=[
            pl.BlockSpec((1, span), whole),
            pl.BlockSpec((OV * OV, BS, BS), lambda i, s, k: (0, 0, 0)),
        ],
        scratch_shapes=[
            pltpu.VMEM((rows, span), jnp.float32),
            pltpu.VMEM((OV * OV, BS, BS), jnp.float32),
            pltpu.VMEM((rows, rows), jnp.bfloat16),
            pltpu.VMEM((rows, rows), jnp.bfloat16),
            pltpu.SemaphoreType.DMA((batch_count * OV,)),
            pltpu.SemaphoreType.DMA((OV * OV,)),
        ],
    )
    density, pair_tiles = pl.pallas_call(
        batch_kernel,
        grid_spec=grid_spec,
        out_shape=[
            jax.ShapeDtypeStruct((1, span), jnp.float32),
            jax.ShapeDtypeStruct((OV * OV, BS, BS), jnp.float32),
        ],
    )(
        source.reshape(-1),
        pick,
        tables,
        tile_values,
        weights.reshape(1, span),
        local_pot.reshape(1, span),
    )
    return density.reshape(batch_count, points), pair_tiles


def body(coeffs, occupation, kept_tiles, tile_slot, blocks, batch_slot, tables, weights, local_pot):
    devices = lax.axis_size("tiles")
    my_index = lax.axis_index("tiles")
    kept_count = kept_tiles.shape[0]
    owned_count = kept_count // devices
    batch_count = tables.shape[0]
    batch_total = batch_slot.shape[0]
    state_count = coeffs.shape[0]
    block_total = coeffs.shape[1] // BS
    points = tables.shape[-1]
    width = OV * BS

    ladder_kept = jnp.arange(kept_count, dtype=jnp.int32)
    slot_kept = jnp.zeros((kept_count,), jnp.int32).at[tile_slot].set(ladder_kept)
    pairs = kept_tiles[slot_kept]
    partial = tile_products(coeffs, occupation, pairs).reshape(devices, owned_count, BS, BS)
    owned = jnp.sum(lax.all_to_all(partial, "tiles", 0, 0, tiled=False), axis=0)
    spread = jnp.broadcast_to(owned[None], (devices, owned_count, BS, BS))
    tile_values = lax.all_to_all(spread, "tiles", 0, 0, tiled=False).reshape(kept_count, BS, BS)

    ladder_batch = jnp.arange(batch_total, dtype=jnp.int32)
    slot_batch = jnp.zeros((batch_total,), jnp.int32).at[batch_slot].set(ladder_batch)
    my_batches = lax.dynamic_slice_in_dim(slot_batch, my_index * batch_count, batch_count)
    my_blocks = blocks[my_batches]
    canon = jnp.sort(my_blocks[0])
    ladder_ov = jnp.arange(OV, dtype=jnp.int32)
    match = my_blocks[:, :, None] == canon[None, None, :]
    source = jnp.sum(jnp.where(match, ladder_ov[None, :, None], 0), axis=1)
    row_hit = pairs[:, 0:1] == canon[None, :]
    col_hit = pairs[:, 1:2] == canon[None, :]
    present = jnp.any(row_hit, axis=1) & jnp.any(col_hit, axis=1)
    row_place = jnp.sum(jnp.where(row_hit, ladder_ov[None, :], 0), axis=1)
    col_place = jnp.sum(jnp.where(col_hit, ladder_ov[None, :], 0), axis=1)
    pair_code = row_place * OV + col_place
    ladder_pair = jnp.arange(OV * OV, dtype=jnp.int32)
    at_pair = present[None, :] & (pair_code[None, :] == ladder_pair[:, None])
    pick = jnp.where(
        jnp.any(at_pair, axis=1), jnp.sum(jnp.where(at_pair, ladder_kept[None, :], 0), axis=1), -1
    )
    density, pair_tiles = batch_terms(source, pick, tables, tile_values, weights, local_pot)
    contrib = jnp.where(present[:, None, None], pair_tiles[pair_code], 0.0)

    terms = contrib.reshape(devices, owned_count, BS, BS)
    matrix = jnp.sum(lax.all_to_all(terms, "tiles", 0, 0, tiled=False), axis=0)
    matrix = matrix.reshape(owned_count, BS * BS)
    return (density, matrix)


def solution(mesh):
    in_specs = (
        P(("groups", "tiles"), None),
        P(("groups", "tiles")),
        P("groups", None),
        P("groups"),
        P("groups", None),
        P("groups"),
        P(("groups", "tiles"), None, None),
        P(("groups", "tiles"), None),
        P(("groups", "tiles"), None),
    )
    out_specs = (P(("groups", "tiles"), None), P(("groups", "tiles"), None))
    return jax.shard_map(body, mesh=mesh, in_specs=in_specs, out_specs=out_specs, check_vma=False)
```

```python
import jax
import jax.numpy as jnp
from jax import lax
from jax.experimental import pallas as pl
from jax.experimental.pallas import tpu as pltpu
from jax.sharding import PartitionSpec as P

BS = 64
OV = 8


def tile_kernel(pairs_ref, *refs):
    group = (len(refs) - 3) // 2
    occ_ref = refs[2 * group]
    out_ref = refs[2 * group + 1]
    tile_ref = refs[2 * group + 2]
    k = pl.program_id(0)
    occ = occ_ref[...]
    for i in range(group):
        row_block = pairs_ref[2 * (group * k + i)]
        col_block = pairs_ref[2 * (group * k + i) + 1]
        left = refs[i][...]
        right = refs[group + i][...] * occ
        left = jnp.where(row_block % 2 == 0, left[:, :BS], left[:, BS:])
        right = jnp.where(col_block % 2 == 0, right[:, :BS], right[:, BS:])
        tile_ref[:, :BS] = lax.dot_general(
            left,
            right,
            (((0,), (0,)), ((), ())),
            precision=lax.Precision.HIGHEST,
            preferred_element_type=jnp.float32,
        )
        out_ref[i, :, :BS] = tile_ref[pl.ds(0, BS // 2, stride=2), :BS]
        out_ref[i, :, BS:] = tile_ref[pl.ds(1, BS // 2, stride=2), :BS]


def tile_products(coeffs, occupation, pairs):
    state_count = coeffs.shape[0]
    kept_count = pairs.shape[0]
    group = next(g for g in (8, 4, 2, 1) if kept_count % g == 0)

    def block_of(i, side):
        return pl.BlockSpec(
            (state_count, 2 * BS), lambda k, p: (0, p[2 * (group * k + i) + side] // 2)
        )

    grid_spec = pltpu.PrefetchScalarGridSpec(
        num_scalar_prefetch=1,
        grid=(kept_count // group,),
        in_specs=[block_of(i, 0) for i in range(group)]
        + [block_of(i, 1) for i in range(group)]
        + [pl.BlockSpec((state_count, 1), lambda k, p: (0, 0))],
        out_specs=pl.BlockSpec((group, BS // 2, 2 * BS), lambda k, p: (k, 0, 0)),
        scratch_shapes=[pltpu.VMEM((BS, 2 * BS), jnp.float32)],
    )
    return pl.pallas_call(
        tile_kernel,
        grid_spec=grid_spec,
        out_shape=jax.ShapeDtypeStruct((kept_count, BS // 2, 2 * BS), jnp.float32),
    )(pairs.reshape(-1), *([coeffs] * (2 * group)), occupation.reshape(state_count, 1))


def split_dot(left, right, dims):
    left_hi = left.astype(jnp.bfloat16)
    left_lo = (left - left_hi.astype(jnp.float32)).astype(jnp.bfloat16)
    right_hi = right.astype(jnp.bfloat16)
    right_lo = (right - right_hi.astype(jnp.float32)).astype(jnp.bfloat16)

    def one(a, b):
        return lax.dot_general(a, b, (dims, ((), ())), preferred_element_type=jnp.float32)

    return one(left_hi, right_hi) + (one(left_hi, right_lo) + one(left_lo, right_hi))


def batch_kernel(
    source_ref, pick_ref, table_hbm, tile_hbm, weight_ref, base_ref,
    density_ref, pair_ref, canon_ref, chunk_ref, perm_ref, stage_ref, dense_hi_ref, dense_lo_ref,
    table_sems, chunk_sems, tile_sems,
):
    half = BS // 2
    lane = 2 * BS
    batch_count, _, points = table_hbm.shape
    copies = []
    for b in range(batch_count):
        for q in range(OV):
            start = pl.multiple_of(source_ref[b * OV + q] * BS, BS)
            copy = pltpu.make_async_copy(
                table_hbm.at[b, pl.ds(start, BS), :],
                canon_ref.at[q * BS:(q + 1) * BS, b * points:(b + 1) * points],
                table_sems.at[b * OV + q],
            )
            copy.start()
            copies.append(copy)
    chunk_copies = []
    for b in range(batch_count):
        for q in range(OV):
            start = pl.multiple_of(source_ref[b * OV + q] * BS, BS)
            for h in range(points // lane):
                c = b * (points // lane) + h
                copy = pltpu.make_async_copy(
                    table_hbm.at[b, pl.ds(start, BS), h * lane:(h + 1) * lane],
                    chunk_ref.at[c, q * BS:(q + 1) * BS, :],
                    chunk_sems.at[c * OV + q],
                )
                copy.start()
                chunk_copies.append(copy)
    for p in range(OV * OV):
        copy = pltpu.make_async_copy(
            tile_hbm.at[jnp.maximum(pick_ref[p], 0)], stage_ref.at[p], tile_sems.at[p]
        )
        copy.start()
        copies.append(copy)
    for copy in copies[batch_count * OV:]:
        copy.wait()
    for q1 in range(OV):
        for q2 in range(OV):
            p = q1 * OV + q2
            tile = jnp.where(pick_ref[p] >= 0, stage_ref[p], 0.0)
            tile_hi = tile.astype(jnp.bfloat16)
            tile_lo = (tile - tile_hi.astype(jnp.float32)).astype(jnp.bfloat16)
            dense_hi_ref[q1 * BS:q1 * BS + half, q2 * BS:(q2 + 1) * BS] = tile_hi[:, :BS]
            dense_hi_ref[q1 * BS + half:(q1 + 1) * BS, q2 * BS:(q2 + 1) * BS] = tile_hi[:, BS:]
            dense_lo_ref[q1 * BS:q1 * BS + half, q2 * BS:(q2 + 1) * BS] = tile_lo[:, :BS]
            dense_lo_ref[q1 * BS + half:(q1 + 1) * BS, q2 * BS:(q2 + 1) * BS] = tile_lo[:, BS:]
    for copy in copies[:batch_count * OV] + chunk_copies:
        copy.wait()
    for c in range(chunk_ref.shape[0]):
        for q in range(OV):
            perm_ref[q * BS:q * BS + half, c * lane:(c + 1) * lane] = chunk_ref[c, pl.ds(q * BS, half, stride=2), :]
            perm_ref[q * BS + half:(q + 1) * BS, c * lane:(c + 1) * lane] = chunk_ref[
                c, pl.ds(q * BS + 1, half, stride=2), :
            ]

    grid = canon_ref[...]
    grid_hi = grid.astype(jnp.bfloat16)
    grid_lo = (grid - grid_hi.astype(jnp.float32)).astype(jnp.bfloat16)

    def nn(a, c):
        return lax.dot_general(a, c, (((1,), (0,)), ((), ())), preferred_element_type=jnp.float32)

    dense_hi = dense_hi_ref[...]
    mixed = nn(dense_hi, grid_hi) + (nn(dense_hi, grid_lo) + nn(dense_lo_ref[...], grid_hi))
    permuted = perm_ref[...]
    density = jnp.sum(permuted * mixed, axis=0, keepdims=True)
    potential = base_ref[...] + density - density * density * density / 6.0
    density_ref[...] = density
    weighted = permuted * (weight_ref[...] * potential)
    terms = split_dot(weighted, grid, ((1,), (1,)))
    for q1 in range(OV):
        for q2 in range(OV):
            pair_ref[q1 * OV + q2, :, :BS] = terms[q1 * BS:q1 * BS + half, q2 * BS:(q2 + 1) * BS]
            pair_ref[q1 * OV + q2, :, BS:] = terms[q1 * BS + half:(q1 + 1) * BS, q2 * BS:(q2 + 1) * BS]


def batch_terms(source, pick, tables, tile_values, weights, local_pot):
    batch_count, rows, points = tables.shape
    span = batch_count * points
    whole = lambda i, s, k: (0, 0)
    grid_spec = pltpu.PrefetchScalarGridSpec(
        num_scalar_prefetch=2,
        grid=(1,),
        in_specs=[
            pl.BlockSpec(memory_space=pl.ANY),
            pl.BlockSpec(memory_space=pl.ANY),
            pl.BlockSpec((1, span), whole),
            pl.BlockSpec((1, span), whole),
        ],
        out_specs=[
            pl.BlockSpec((1, span), whole),
            pl.BlockSpec((OV * OV, BS // 2, 2 * BS), lambda i, s, k: (0, 0, 0)),
        ],
        scratch_shapes=[
            pltpu.VMEM((rows, span), jnp.float32),
            pltpu.VMEM((span // (2 * BS), rows, 2 * BS), jnp.float32),
            pltpu.VMEM((rows, span), jnp.float32),
            pltpu.VMEM((OV * OV, BS // 2, 2 * BS), jnp.float32),
            pltpu.VMEM((rows, rows), jnp.bfloat16),
            pltpu.VMEM((rows, rows), jnp.bfloat16),
            pltpu.SemaphoreType.DMA((batch_count * OV,)),
            pltpu.SemaphoreType.DMA((span // (2 * BS) * OV,)),
            pltpu.SemaphoreType.DMA((OV * OV,)),
        ],
    )
    density, pair_tiles = pl.pallas_call(
        batch_kernel,
        grid_spec=grid_spec,
        out_shape=[
            jax.ShapeDtypeStruct((1, span), jnp.float32),
            jax.ShapeDtypeStruct((OV * OV, BS // 2, 2 * BS), jnp.float32),
        ],
    )(
        source.reshape(-1),
        pick,
        tables,
        tile_values,
        weights.reshape(1, span),
        local_pot.reshape(1, span),
    )
    return density.reshape(batch_count, points), pair_tiles


def body(coeffs, occupation, kept_tiles, tile_slot, blocks, batch_slot, tables, weights, local_pot):
    devices = lax.axis_size("tiles")
    my_index = lax.axis_index("tiles")
    kept_count = kept_tiles.shape[0]
    owned_count = kept_count // devices
    batch_count = tables.shape[0]
    batch_total = batch_slot.shape[0]
    state_count = coeffs.shape[0]
    block_total = coeffs.shape[1] // BS
    points = tables.shape[-1]
    width = OV * BS

    ladder_kept = jnp.arange(kept_count, dtype=jnp.int32)
    slot_kept = jnp.zeros((kept_count,), jnp.int32).at[tile_slot].set(ladder_kept)
    pairs = kept_tiles[slot_kept]
    partial = tile_products(coeffs, occupation, pairs).reshape(devices, owned_count, BS // 2, 2 * BS)
    owned = jnp.sum(lax.all_to_all(partial, "tiles", 0, 0, tiled=False), axis=0)
    spread = jnp.broadcast_to(owned[None], (devices, owned_count, BS // 2, 2 * BS))
    tile_values = lax.all_to_all(spread, "tiles", 0, 0, tiled=False).reshape(
        kept_count, BS // 2, 2 * BS
    )

    ladder_batch = jnp.arange(batch_total, dtype=jnp.int32)
    slot_batch = jnp.zeros((batch_total,), jnp.int32).at[batch_slot].set(ladder_batch)
    my_batches = lax.dynamic_slice_in_dim(slot_batch, my_index * batch_count, batch_count)
    my_blocks = blocks[my_batches]
    canon = jnp.sort(my_blocks[0])
    ladder_ov = jnp.arange(OV, dtype=jnp.int32)
    match = my_blocks[:, :, None] == canon[None, None, :]
    source = jnp.sum(jnp.where(match, ladder_ov[None, :, None], 0), axis=1)
    row_hit = pairs[:, 0:1] == canon[None, :]
    col_hit = pairs[:, 1:2] == canon[None, :]
    present = jnp.any(row_hit, axis=1) & jnp.any(col_hit, axis=1)
    row_place = jnp.sum(jnp.where(row_hit, ladder_ov[None, :], 0), axis=1)
    col_place = jnp.sum(jnp.where(col_hit, ladder_ov[None, :], 0), axis=1)
    pair_code = row_place * OV + col_place
    ladder_pair = jnp.arange(OV * OV, dtype=jnp.int32)
    at_pair = present[None, :] & (pair_code[None, :] == ladder_pair[:, None])
    pick = jnp.where(
        jnp.any(at_pair, axis=1), jnp.sum(jnp.where(at_pair, ladder_kept[None, :], 0), axis=1), -1
    )
    density, pair_tiles = batch_terms(source, pick, tables, tile_values, weights, local_pot)
    contrib = jnp.where(present[:, None, None], pair_tiles[pair_code], 0.0)

    terms = contrib.reshape(devices, owned_count, BS // 2, 2 * BS)
    matrix = jnp.sum(lax.all_to_all(terms, "tiles", 0, 0, tiled=False), axis=0)
    matrix = matrix.reshape(owned_count, BS * BS)
    return (density, matrix)


def solution(mesh):
    in_specs = (
        P(("groups", "tiles"), None),
        P(("groups", "tiles")),
        P("groups", None),
        P("groups"),
        P("groups", None),
        P("groups"),
        P(("groups", "tiles"), None, None),
        P(("groups", "tiles"), None),
        P(("groups", "tiles"), None),
    )
    out_specs = (P(("groups", "tiles"), None), P(("groups", "tiles"), None))
    return jax.shard_map(body, mesh=mesh, in_specs=in_specs, out_specs=out_specs, check_vma=False)
```

```python
import jax
import jax.numpy as jnp
from jax import lax
from jax.experimental import pallas as pl
from jax.experimental.pallas import tpu as pltpu
from jax.sharding import PartitionSpec as P

BS = 64
OV = 8


def tile_kernel(pairs_ref, *refs):
    group = (len(refs) - 2) // 2
    occ_ref = refs[2 * group]
    out_ref = refs[2 * group + 1]
    k = pl.program_id(0)
    occ = occ_ref[...]
    for i in range(group):
        row_block = pairs_ref[2 * (group * k + i)]
        col_block = pairs_ref[2 * (group * k + i) + 1]
        left = refs[i][...]
        right = refs[group + i][...] * occ
        left = jnp.where(row_block % 2 == 0, left[:, :BS], left[:, BS:])
        right = jnp.where(col_block % 2 == 0, right[:, :BS], right[:, BS:])
        out_ref[i] = lax.dot_general(
            left,
            right,
            (((0,), (0,)), ((), ())),
            precision=lax.Precision.HIGHEST,
            preferred_element_type=jnp.float32,
        )


def tile_products(coeffs, occupation, pairs):
    state_count = coeffs.shape[0]
    kept_count = pairs.shape[0]
    group = next(g for g in (8, 4, 2, 1) if kept_count % g == 0)

    def block_of(i, side):
        return pl.BlockSpec(
            (state_count, 2 * BS), lambda k, p: (0, p[2 * (group * k + i) + side] // 2)
        )

    grid_spec = pltpu.PrefetchScalarGridSpec(
        num_scalar_prefetch=1,
        grid=(kept_count // group,),
        in_specs=[block_of(i, 0) for i in range(group)]
        + [block_of(i, 1) for i in range(group)]
        + [pl.BlockSpec((state_count, 1), lambda k, p: (0, 0))],
        out_specs=pl.BlockSpec((group, BS, BS), lambda k, p: (k, 0, 0)),
    )
    return pl.pallas_call(
        tile_kernel,
        grid_spec=grid_spec,
        out_shape=jax.ShapeDtypeStruct((kept_count, BS, BS), jnp.float32),
    )(pairs.reshape(-1), *([coeffs] * (2 * group)), occupation.reshape(state_count, 1))


def split_dot(left, right, dims):
    left_hi = left.astype(jnp.bfloat16)
    left_lo = (left - left_hi.astype(jnp.float32)).astype(jnp.bfloat16)
    right_hi = right.astype(jnp.bfloat16)
    right_lo = (right - right_hi.astype(jnp.float32)).astype(jnp.bfloat16)

    def one(a, b):
        return lax.dot_general(a, b, (dims, ((), ())), preferred_element_type=jnp.float32)

    return one(left_hi, right_hi) + (one(left_hi, right_lo) + one(left_lo, right_hi))


def batch_kernel(
    source_ref, pick_ref, table_hbm, tile_hbm, weight_ref, base_ref,
    density_ref, pair_ref, canon_ref, chunk_ref, perm_ref, stage_ref, dense_hi_ref, dense_lo_ref,
    table_sems, chunk_sems, tile_sems,
):
    half = BS // 2
    lane = 2 * BS
    batch_count, _, points = table_hbm.shape
    copies = []
    for b in range(batch_count):
        for q in range(OV):
            start = pl.multiple_of(source_ref[b * OV + q] * BS, BS)
            copy = pltpu.make_async_copy(
                table_hbm.at[b, pl.ds(start, BS), :],
                canon_ref.at[q * BS:(q + 1) * BS, b * points:(b + 1) * points],
                table_sems.at[b * OV + q],
            )
            copy.start()
            copies.append(copy)
    chunk_copies = []
    for b in range(batch_count):
        for q in range(OV):
            start = pl.multiple_of(source_ref[b * OV + q] * BS, BS)
            for h in range(points // lane):
                c = b * (points // lane) + h
                copy = pltpu.make_async_copy(
                    table_hbm.at[b, pl.ds(start, BS), h * lane:(h + 1) * lane],
                    chunk_ref.at[c, q * BS:(q + 1) * BS, :],
                    chunk_sems.at[c * OV + q],
                )
                copy.start()
                chunk_copies.append(copy)
    for p in range(OV * OV):
        copy = pltpu.make_async_copy(
            tile_hbm.at[jnp.maximum(pick_ref[p], 0)], stage_ref.at[p], tile_sems.at[p]
        )
        copy.start()
        copies.append(copy)
    for copy in copies[batch_count * OV:]:
        copy.wait()
    for q1 in range(OV):
        for q2 in range(OV):
            p = q1 * OV + q2
            tile = jnp.where(pick_ref[p] >= 0, stage_ref[p], 0.0)
            tile_hi = tile.astype(jnp.bfloat16)
            tile_lo = (tile - tile_hi.astype(jnp.float32)).astype(jnp.bfloat16)
            dense_hi_ref[q1 * BS:q1 * BS + half, q2 * BS:(q2 + 1) * BS] = tile_hi[:, :BS]
            dense_hi_ref[q1 * BS + half:(q1 + 1) * BS, q2 * BS:(q2 + 1) * BS] = tile_hi[:, BS:]
            dense_lo_ref[q1 * BS:q1 * BS + half, q2 * BS:(q2 + 1) * BS] = tile_lo[:, :BS]
            dense_lo_ref[q1 * BS + half:(q1 + 1) * BS, q2 * BS:(q2 + 1) * BS] = tile_lo[:, BS:]
    for copy in copies[:batch_count * OV] + chunk_copies:
        copy.wait()
    for c in range(chunk_ref.shape[0]):
        for q in range(OV):
            perm_ref[q * BS:q * BS + half, c * lane:(c + 1) * lane] = chunk_ref[c, pl.ds(q * BS, half, stride=2), :]
            perm_ref[q * BS + half:(q + 1) * BS, c * lane:(c + 1) * lane] = chunk_ref[
                c, pl.ds(q * BS + 1, half, stride=2), :
            ]

    grid = canon_ref[...]
    grid_hi = grid.astype(jnp.bfloat16)
    grid_lo = (grid - grid_hi.astype(jnp.float32)).astype(jnp.bfloat16)

    def nn(a, c):
        return lax.dot_general(a, c, (((1,), (0,)), ((), ())), preferred_element_type=jnp.float32)

    dense_hi = dense_hi_ref[...]
    mixed = nn(dense_hi, grid_hi) + (nn(dense_hi, grid_lo) + nn(dense_lo_ref[...], grid_hi))
    permuted = perm_ref[...]
    density = jnp.sum(permuted * mixed, axis=0, keepdims=True)
    potential = base_ref[...] + density - density * density * density / 6.0
    density_ref[...] = density
    weighted = permuted * (weight_ref[...] * potential)
    terms = split_dot(weighted, grid, ((1,), (1,)))
    for q1 in range(OV):
        for q2 in range(OV):
            pair_ref[q1 * OV + q2, :, :BS] = terms[q1 * BS:q1 * BS + half, q2 * BS:(q2 + 1) * BS]
            pair_ref[q1 * OV + q2, :, BS:] = terms[q1 * BS + half:(q1 + 1) * BS, q2 * BS:(q2 + 1) * BS]


def batch_terms(source, pick, tables, tile_values, weights, local_pot):
    batch_count, rows, points = tables.shape
    span = batch_count * points
    whole = lambda i, s, k: (0, 0)
    grid_spec = pltpu.PrefetchScalarGridSpec(
        num_scalar_prefetch=2,
        grid=(1,),
        in_specs=[
            pl.BlockSpec(memory_space=pl.ANY),
            pl.BlockSpec(memory_space=pl.ANY),
            pl.BlockSpec((1, span), whole),
            pl.BlockSpec((1, span), whole),
        ],
        out_specs=[
            pl.BlockSpec((1, span), whole),
            pl.BlockSpec((OV * OV, BS // 2, 2 * BS), lambda i, s, k: (0, 0, 0)),
        ],
        scratch_shapes=[
            pltpu.VMEM((rows, span), jnp.float32),
            pltpu.VMEM((span // (2 * BS), rows, 2 * BS), jnp.float32),
            pltpu.VMEM((rows, span), jnp.float32),
            pltpu.VMEM((OV * OV, BS // 2, 2 * BS), jnp.float32),
            pltpu.VMEM((rows, rows), jnp.bfloat16),
            pltpu.VMEM((rows, rows), jnp.bfloat16),
            pltpu.SemaphoreType.DMA((batch_count * OV,)),
            pltpu.SemaphoreType.DMA((span // (2 * BS) * OV,)),
            pltpu.SemaphoreType.DMA((OV * OV,)),
        ],
    )
    density, pair_tiles = pl.pallas_call(
        batch_kernel,
        grid_spec=grid_spec,
        out_shape=[
            jax.ShapeDtypeStruct((1, span), jnp.float32),
            jax.ShapeDtypeStruct((OV * OV, BS // 2, 2 * BS), jnp.float32),
        ],
    )(
        source.reshape(-1),
        pick,
        tables,
        tile_values,
        weights.reshape(1, span),
        local_pot.reshape(1, span),
    )
    return density.reshape(batch_count, points), pair_tiles


def body(coeffs, occupation, kept_tiles, tile_slot, blocks, batch_slot, tables, weights, local_pot):
    devices = lax.axis_size("tiles")
    my_index = lax.axis_index("tiles")
    kept_count = kept_tiles.shape[0]
    owned_count = kept_count // devices
    batch_count = tables.shape[0]
    batch_total = batch_slot.shape[0]
    state_count = coeffs.shape[0]
    block_total = coeffs.shape[1] // BS
    points = tables.shape[-1]
    width = OV * BS

    ladder_kept = jnp.arange(kept_count, dtype=jnp.int32)
    slot_kept = jnp.zeros((kept_count,), jnp.int32).at[tile_slot].set(ladder_kept)
    pairs = kept_tiles[slot_kept]
    partial = tile_products(coeffs, occupation, pairs).reshape(devices, owned_count, BS // 2, 2 * BS)
    owned = jnp.sum(lax.all_to_all(partial, "tiles", 0, 0, tiled=False), axis=0)
    spread = jnp.broadcast_to(owned[None], (devices, owned_count, BS // 2, 2 * BS))
    tile_values = lax.all_to_all(spread, "tiles", 0, 0, tiled=False).reshape(
        kept_count, BS // 2, 2 * BS
    )

    ladder_batch = jnp.arange(batch_total, dtype=jnp.int32)
    slot_batch = jnp.zeros((batch_total,), jnp.int32).at[batch_slot].set(ladder_batch)
    my_batches = lax.dynamic_slice_in_dim(slot_batch, my_index * batch_count, batch_count)
    my_blocks = blocks[my_batches]
    canon = jnp.sort(my_blocks[0])
    ladder_ov = jnp.arange(OV, dtype=jnp.int32)
    match = my_blocks[:, :, None] == canon[None, None, :]
    source = jnp.sum(jnp.where(match, ladder_ov[None, :, None], 0), axis=1)
    row_hit = pairs[:, 0:1] == canon[None, :]
    col_hit = pairs[:, 1:2] == canon[None, :]
    present = jnp.any(row_hit, axis=1) & jnp.any(col_hit, axis=1)
    row_place = jnp.sum(jnp.where(row_hit, ladder_ov[None, :], 0), axis=1)
    col_place = jnp.sum(jnp.where(col_hit, ladder_ov[None, :], 0), axis=1)
    pair_code = row_place * OV + col_place
    ladder_pair = jnp.arange(OV * OV, dtype=jnp.int32)
    at_pair = present[None, :] & (pair_code[None, :] == ladder_pair[:, None])
    pick = jnp.where(
        jnp.any(at_pair, axis=1), jnp.sum(jnp.where(at_pair, ladder_kept[None, :], 0), axis=1), -1
    )
    density, pair_tiles = batch_terms(source, pick, tables, tile_values, weights, local_pot)
    contrib = jnp.where(present[:, None, None], pair_tiles[pair_code], 0.0)

    terms = contrib.reshape(devices, owned_count, BS // 2, 2 * BS)
    matrix = jnp.sum(lax.all_to_all(terms, "tiles", 0, 0, tiled=False), axis=0)
    matrix = matrix.reshape(owned_count, BS * BS)
    return (density, matrix)


def solution(mesh):
    in_specs = (
        P(("groups", "tiles"), None),
        P(("groups", "tiles")),
        P("groups", None),
        P("groups"),
        P("groups", None),
        P("groups"),
        P(("groups", "tiles"), None, None),
        P(("groups", "tiles"), None),
        P(("groups", "tiles"), None),
    )
    out_specs = (P(("groups", "tiles"), None), P(("groups", "tiles"), None))
    return jax.shard_map(body, mesh=mesh, in_specs=in_specs, out_specs=out_specs, check_vma=False)
```

```python
import jax
import jax.numpy as jnp
from jax import lax
from jax.experimental import pallas as pl
from jax.experimental.pallas import tpu as pltpu
from jax.sharding import PartitionSpec as P

BS = 64
OV = 8


def tile_kernel(pairs_ref, *refs):
    group = (len(refs) - 2) // 2
    occ_ref = refs[2 * group]
    out_ref = refs[2 * group + 1]
    k = pl.program_id(0)
    occ = occ_ref[...]
    for i in range(group):
        row_block = pairs_ref[2 * (group * k + i)]
        col_block = pairs_ref[2 * (group * k + i) + 1]
        left = refs[i][...]
        right = refs[group + i][...] * occ
        left = jnp.where(row_block % 2 == 0, left[:, :BS], left[:, BS:])
        right = jnp.where(col_block % 2 == 0, right[:, :BS], right[:, BS:])
        out_ref[i] = lax.dot_general(
            left,
            right,
            (((0,), (0,)), ((), ())),
            precision=lax.Precision.HIGHEST,
            preferred_element_type=jnp.float32,
        )


def tile_products(coeffs, occupation, pairs):
    state_count = coeffs.shape[0]
    kept_count = pairs.shape[0]
    group = next(g for g in (8, 4, 2, 1) if kept_count % g == 0)

    def block_of(i, side):
        return pl.BlockSpec(
            (state_count, 2 * BS), lambda k, p: (0, p[2 * (group * k + i) + side] // 2)
        )

    grid_spec = pltpu.PrefetchScalarGridSpec(
        num_scalar_prefetch=1,
        grid=(kept_count // group,),
        in_specs=[block_of(i, 0) for i in range(group)]
        + [block_of(i, 1) for i in range(group)]
        + [pl.BlockSpec((state_count, 1), lambda k, p: (0, 0))],
        out_specs=pl.BlockSpec((group, BS, BS), lambda k, p: (k, 0, 0)),
    )
    return pl.pallas_call(
        tile_kernel,
        grid_spec=grid_spec,
        out_shape=jax.ShapeDtypeStruct((kept_count, BS, BS), jnp.float32),
    )(pairs.reshape(-1), *([coeffs] * (2 * group)), occupation.reshape(state_count, 1))


def split_dot(left, right, dims):
    left_hi = left.astype(jnp.bfloat16)
    left_lo = (left - left_hi.astype(jnp.float32)).astype(jnp.bfloat16)
    right_hi = right.astype(jnp.bfloat16)
    right_lo = (right - right_hi.astype(jnp.float32)).astype(jnp.bfloat16)

    def one(a, b):
        return lax.dot_general(a, b, (dims, ((), ())), preferred_element_type=jnp.float32)

    return one(left_hi, right_hi) + (one(left_hi, right_lo) + one(left_lo, right_hi))


def prep_kernel(source_ref, table_hbm, hi_ref, lo_ref, perm_ref, canon_ref, chunk_ref, table_sems, chunk_sems):
    half = BS // 2
    lane = 2 * BS
    batch_count, _, points = table_hbm.shape
    copies = []
    chunk_copies = []
    for b in range(batch_count):
        for q in range(OV):
            start = pl.multiple_of(source_ref[b * OV + q] * BS, BS)
            copy = pltpu.make_async_copy(
                table_hbm.at[b, pl.ds(start, BS), :],
                canon_ref.at[q * BS:(q + 1) * BS, b * points:(b + 1) * points],
                table_sems.at[b * OV + q],
            )
            copy.start()
            copies.append(copy)
            for h in range(points // lane):
                c = b * (points // lane) + h
                copy = pltpu.make_async_copy(
                    table_hbm.at[b, pl.ds(start, BS), h * lane:(h + 1) * lane],
                    chunk_ref.at[c, q * BS:(q + 1) * BS, :],
                    chunk_sems.at[c * OV + q],
                )
                copy.start()
                chunk_copies.append(copy)
    for copy in copies:
        copy.wait()
    grid = canon_ref[...]
    grid_hi = grid.astype(jnp.bfloat16)
    hi_ref[...] = grid_hi
    lo_ref[...] = (grid - grid_hi.astype(jnp.float32)).astype(jnp.bfloat16)
    for copy in chunk_copies:
        copy.wait()
    for c in range(chunk_ref.shape[0]):
        for q in range(OV):
            perm_ref[q * BS:q * BS + half, c * lane:(c + 1) * lane] = chunk_ref[c, pl.ds(q * BS, half, stride=2), :]
            perm_ref[q * BS + half:(q + 1) * BS, c * lane:(c + 1) * lane] = chunk_ref[
                c, pl.ds(q * BS + 1, half, stride=2), :
            ]


def prep_tables(source, tables):
    batch_count, rows, points = tables.shape
    span = batch_count * points
    whole = lambda i, s: (0, 0)
    grid_spec = pltpu.PrefetchScalarGridSpec(
        num_scalar_prefetch=1,
        grid=(1,),
        in_specs=[pl.BlockSpec(memory_space=pl.ANY)],
        out_specs=[
            pl.BlockSpec((rows, span), whole),
            pl.BlockSpec((rows, span), whole),
            pl.BlockSpec((rows, span), whole),
        ],
        scratch_shapes=[
            pltpu.VMEM((rows, span), jnp.float32),
            pltpu.VMEM((span // (2 * BS), rows, 2 * BS), jnp.float32),
            pltpu.SemaphoreType.DMA((batch_count * OV,)),
            pltpu.SemaphoreType.DMA((span // (2 * BS) * OV,)),
        ],
    )
    return pl.pallas_call(
        prep_kernel,
        grid_spec=grid_spec,
        out_shape=[
            jax.ShapeDtypeStruct((rows, span), jnp.bfloat16),
            jax.ShapeDtypeStruct((rows, span), jnp.bfloat16),
            jax.ShapeDtypeStruct((rows, span), jnp.float32),
        ],
    )(source.reshape(-1), tables)


def batch_kernel(
    pick_ref, hi_ref, lo_ref, perm_ref, tile_hbm, weight_ref, base_ref,
    density_ref, pair_ref, stage_ref, dense_hi_ref, dense_lo_ref, tile_sems,
):
    half = BS // 2
    copies = []
    for p in range(OV * OV):
        copy = pltpu.make_async_copy(
            tile_hbm.at[jnp.maximum(pick_ref[p], 0)], stage_ref.at[p], tile_sems.at[p]
        )
        copy.start()
        copies.append(copy)
    for copy in copies:
        copy.wait()
    for q1 in range(OV):
        for q2 in range(OV):
            p = q1 * OV + q2
            tile = jnp.where(pick_ref[p] >= 0, stage_ref[p], 0.0)
            tile_hi = tile.astype(jnp.bfloat16)
            tile_lo = (tile - tile_hi.astype(jnp.float32)).astype(jnp.bfloat16)
            dense_hi_ref[q1 * BS:q1 * BS + half, q2 * BS:(q2 + 1) * BS] = tile_hi[:, :BS]
            dense_hi_ref[q1 * BS + half:(q1 + 1) * BS, q2 * BS:(q2 + 1) * BS] = tile_hi[:, BS:]
            dense_lo_ref[q1 * BS:q1 * BS + half, q2 * BS:(q2 + 1) * BS] = tile_lo[:, :BS]
            dense_lo_ref[q1 * BS + half:(q1 + 1) * BS, q2 * BS:(q2 + 1) * BS] = tile_lo[:, BS:]

    def dot(a, c, dims):
        return lax.dot_general(a, c, (dims, ((), ())), preferred_element_type=jnp.float32)

    grid_hi = hi_ref[...]
    grid_lo = lo_ref[...]
    dense_hi = dense_hi_ref[...]
    nn = ((1,), (0,))
    mixed = dot(dense_hi, grid_hi, nn) + (dot(dense_hi, grid_lo, nn) + dot(dense_lo_ref[...], grid_hi, nn))
    permuted = perm_ref[...]
    density = jnp.sum(permuted * mixed, axis=0, keepdims=True)
    potential = base_ref[...] + density - density * density * density / 6.0
    density_ref[...] = density
    weighted = permuted * (weight_ref[...] * potential)
    weighted_hi = weighted.astype(jnp.bfloat16)
    weighted_lo = (weighted - weighted_hi.astype(jnp.float32)).astype(jnp.bfloat16)
    nt = ((1,), (1,))
    terms = dot(weighted_hi, grid_hi, nt) + (dot(weighted_hi, grid_lo, nt) + dot(weighted_lo, grid_hi, nt))
    for q1 in range(OV):
        for q2 in range(OV):
            pair_ref[q1 * OV + q2, :, :BS] = terms[q1 * BS:q1 * BS + half, q2 * BS:(q2 + 1) * BS]
            pair_ref[q1 * OV + q2, :, BS:] = terms[q1 * BS + half:(q1 + 1) * BS, q2 * BS:(q2 + 1) * BS]


def batch_terms(source, pick, tables, tile_values, weights, local_pot):
    batch_count, rows, points = tables.shape
    span = batch_count * points
    grid_hi, grid_lo, permuted = prep_tables(source, tables)
    whole = lambda i, k: (0, 0)
    grid_spec = pltpu.PrefetchScalarGridSpec(
        num_scalar_prefetch=1,
        grid=(1,),
        in_specs=[
            pl.BlockSpec((rows, span), whole),
            pl.BlockSpec((rows, span), whole),
            pl.BlockSpec((rows, span), whole),
            pl.BlockSpec(memory_space=pl.ANY),
            pl.BlockSpec((1, span), whole),
            pl.BlockSpec((1, span), whole),
        ],
        out_specs=[
            pl.BlockSpec((1, span), whole),
            pl.BlockSpec((OV * OV, BS // 2, 2 * BS), lambda i, k: (0, 0, 0)),
        ],
        scratch_shapes=[
            pltpu.VMEM((OV * OV, BS // 2, 2 * BS), jnp.float32),
            pltpu.VMEM((rows, rows), jnp.bfloat16),
            pltpu.VMEM((rows, rows), jnp.bfloat16),
            pltpu.SemaphoreType.DMA((OV * OV,)),
        ],
    )
    density, pair_tiles = pl.pallas_call(
        batch_kernel,
        grid_spec=grid_spec,
        out_shape=[
            jax.ShapeDtypeStruct((1, span), jnp.float32),
            jax.ShapeDtypeStruct((OV * OV, BS // 2, 2 * BS), jnp.float32),
        ],
    )(
        pick,
        grid_hi,
        grid_lo,
        permuted,
        tile_values,
        weights.reshape(1, span),
        local_pot.reshape(1, span),
    )
    return density.reshape(batch_count, points), pair_tiles


def body(coeffs, occupation, kept_tiles, tile_slot, blocks, batch_slot, tables, weights, local_pot):
    devices = lax.axis_size("tiles")
    my_index = lax.axis_index("tiles")
    kept_count = kept_tiles.shape[0]
    owned_count = kept_count // devices
    batch_count = tables.shape[0]
    batch_total = batch_slot.shape[0]
    state_count = coeffs.shape[0]
    block_total = coeffs.shape[1] // BS
    points = tables.shape[-1]
    width = OV * BS

    ladder_kept = jnp.arange(kept_count, dtype=jnp.int32)
    slot_kept = jnp.zeros((kept_count,), jnp.int32).at[tile_slot].set(ladder_kept)
    pairs = kept_tiles[slot_kept]
    partial = tile_products(coeffs, occupation, pairs).reshape(devices, owned_count, BS // 2, 2 * BS)
    owned = jnp.sum(lax.all_to_all(partial, "tiles", 0, 0, tiled=False), axis=0)
    spread = jnp.broadcast_to(owned[None], (devices, owned_count, BS // 2, 2 * BS))
    tile_values = lax.all_to_all(spread, "tiles", 0, 0, tiled=False).reshape(
        kept_count, BS // 2, 2 * BS
    )

    ladder_batch = jnp.arange(batch_total, dtype=jnp.int32)
    slot_batch = jnp.zeros((batch_total,), jnp.int32).at[batch_slot].set(ladder_batch)
    my_batches = lax.dynamic_slice_in_dim(slot_batch, my_index * batch_count, batch_count)
    my_blocks = blocks[my_batches]
    canon = jnp.sort(my_blocks[0])
    ladder_ov = jnp.arange(OV, dtype=jnp.int32)
    match = my_blocks[:, :, None] == canon[None, None, :]
    source = jnp.sum(jnp.where(match, ladder_ov[None, :, None], 0), axis=1)
    row_hit = pairs[:, 0:1] == canon[None, :]
    col_hit = pairs[:, 1:2] == canon[None, :]
    present = jnp.any(row_hit, axis=1) & jnp.any(col_hit, axis=1)
    row_place = jnp.sum(jnp.where(row_hit, ladder_ov[None, :], 0), axis=1)
    col_place = jnp.sum(jnp.where(col_hit, ladder_ov[None, :], 0), axis=1)
    pair_code = row_place * OV + col_place
    ladder_pair = jnp.arange(OV * OV, dtype=jnp.int32)
    at_pair = present[None, :] & (pair_code[None, :] == ladder_pair[:, None])
    pick = jnp.where(
        jnp.any(at_pair, axis=1), jnp.sum(jnp.where(at_pair, ladder_kept[None, :], 0), axis=1), -1
    )
    density, pair_tiles = batch_terms(source, pick, tables, tile_values, weights, local_pot)
    contrib = jnp.where(present[:, None, None], pair_tiles[pair_code], 0.0)

    terms = contrib.reshape(devices, owned_count, BS // 2, 2 * BS)
    matrix = jnp.sum(lax.all_to_all(terms, "tiles", 0, 0, tiled=False), axis=0)
    matrix = matrix.reshape(owned_count, BS * BS)
    return (density, matrix)


def solution(mesh):
    in_specs = (
        P(("groups", "tiles"), None),
        P(("groups", "tiles")),
        P("groups", None),
        P("groups"),
        P("groups", None),
        P("groups"),
        P(("groups", "tiles"), None, None),
        P(("groups", "tiles"), None),
        P(("groups", "tiles"), None),
    )
    out_specs = (P(("groups", "tiles"), None), P(("groups", "tiles"), None))
    return jax.shard_map(body, mesh=mesh, in_specs=in_specs, out_specs=out_specs, check_vma=False)
```

```python
import jax
import jax.numpy as jnp
from jax import lax
from jax.experimental import pallas as pl
from jax.experimental.pallas import tpu as pltpu
from jax.sharding import PartitionSpec as P

BS = 64
OV = 8


def tile_kernel(pairs_ref, *refs):
    group = (len(refs) - 2) // 2
    occ_ref = refs[2 * group]
    out_ref = refs[2 * group + 1]
    k = pl.program_id(0)
    occ = occ_ref[...]
    for i in range(group):
        row_block = pairs_ref[2 * (group * k + i)]
        col_block = pairs_ref[2 * (group * k + i) + 1]
        left = refs[i][...]
        right = refs[group + i][...] * occ
        left = jnp.where(row_block % 2 == 0, left[:, :BS], left[:, BS:])
        right = jnp.where(col_block % 2 == 0, right[:, :BS], right[:, BS:])
        out_ref[i] = lax.dot_general(
            left,
            right,
            (((0,), (0,)), ((), ())),
            precision=lax.Precision.HIGHEST,
            preferred_element_type=jnp.float32,
        )


def tile_products(coeffs, occupation, pairs):
    state_count = coeffs.shape[0]
    kept_count = pairs.shape[0]
    group = next(g for g in (8, 4, 2, 1) if kept_count % g == 0)

    def block_of(i, side):
        return pl.BlockSpec(
            (state_count, 2 * BS), lambda k, p: (0, p[2 * (group * k + i) + side] // 2)
        )

    grid_spec = pltpu.PrefetchScalarGridSpec(
        num_scalar_prefetch=1,
        grid=(kept_count // group,),
        in_specs=[block_of(i, 0) for i in range(group)]
        + [block_of(i, 1) for i in range(group)]
        + [pl.BlockSpec((state_count, 1), lambda k, p: (0, 0))],
        out_specs=pl.BlockSpec((group, BS, BS), lambda k, p: (k, 0, 0)),
    )
    return pl.pallas_call(
        tile_kernel,
        grid_spec=grid_spec,
        out_shape=jax.ShapeDtypeStruct((kept_count, BS, BS), jnp.float32),
    )(pairs.reshape(-1), *([coeffs] * (2 * group)), occupation.reshape(state_count, 1))


def split_dot(left, right, dims):
    left_hi = left.astype(jnp.bfloat16)
    left_lo = (left - left_hi.astype(jnp.float32)).astype(jnp.bfloat16)
    right_hi = right.astype(jnp.bfloat16)
    right_lo = (right - right_hi.astype(jnp.float32)).astype(jnp.bfloat16)

    def one(a, b):
        return lax.dot_general(a, b, (dims, ((), ())), preferred_element_type=jnp.float32)

    return one(left_hi, right_hi) + (one(left_hi, right_lo) + one(left_lo, right_hi))


def prep_kernel(source_ref, table_hbm, hi_ref, lo_ref, perm_ref, canon_ref, chunk_ref, table_sems, chunk_sems):
    half = BS // 2
    lane = 2 * BS
    batch_count, _, points = table_hbm.shape
    copies = []
    chunk_copies = []
    for b in range(batch_count):
        for q in range(OV):
            start = pl.multiple_of(source_ref[b * OV + q] * BS, BS)
            copy = pltpu.make_async_copy(
                table_hbm.at[b, pl.ds(start, BS), :],
                canon_ref.at[q * BS:(q + 1) * BS, b * points:(b + 1) * points],
                table_sems.at[b * OV + q],
            )
            copy.start()
            copies.append(copy)
            for h in range(points // lane):
                c = b * (points // lane) + h
                copy = pltpu.make_async_copy(
                    table_hbm.at[b, pl.ds(start, BS), h * lane:(h + 1) * lane],
                    chunk_ref.at[c, q * BS:(q + 1) * BS, :],
                    chunk_sems.at[c * OV + q],
                )
                copy.start()
                chunk_copies.append(copy)
    for copy in copies:
        copy.wait()
    grid = canon_ref[...]
    grid_hi = grid.astype(jnp.bfloat16)
    hi_ref[...] = grid_hi
    lo_ref[...] = (grid - grid_hi.astype(jnp.float32)).astype(jnp.bfloat16)
    for copy in chunk_copies:
        copy.wait()
    for c in range(chunk_ref.shape[0]):
        for q in range(OV):
            perm_ref[q * BS:q * BS + half, c * lane:(c + 1) * lane] = chunk_ref[c, pl.ds(q * BS, half, stride=2), :]
            perm_ref[q * BS + half:(q + 1) * BS, c * lane:(c + 1) * lane] = chunk_ref[
                c, pl.ds(q * BS + 1, half, stride=2), :
            ]


def prep_tables(source, tables):
    batch_count, rows, points = tables.shape
    span = batch_count * points
    whole = lambda i, s: (0, 0)
    grid_spec = pltpu.PrefetchScalarGridSpec(
        num_scalar_prefetch=1,
        grid=(1,),
        in_specs=[pl.BlockSpec(memory_space=pl.ANY)],
        out_specs=[
            pl.BlockSpec((rows, span), whole),
            pl.BlockSpec((rows, span), whole),
            pl.BlockSpec((rows, span), whole),
        ],
        scratch_shapes=[
            pltpu.VMEM((rows, span), jnp.float32),
            pltpu.VMEM((span // (2 * BS), rows, 2 * BS), jnp.float32),
            pltpu.SemaphoreType.DMA((batch_count * OV,)),
            pltpu.SemaphoreType.DMA((span // (2 * BS) * OV,)),
        ],
    )
    return pl.pallas_call(
        prep_kernel,
        grid_spec=grid_spec,
        out_shape=[
            jax.ShapeDtypeStruct((rows, span), jnp.bfloat16),
            jax.ShapeDtypeStruct((rows, span), jnp.bfloat16),
            jax.ShapeDtypeStruct((rows, span), jnp.float32),
        ],
    )(source.reshape(-1), tables)


def batch_kernel(
    pick_ref, code_ref, hi_ref, lo_ref, perm_ref, tile_hbm, weight_ref, base_ref,
    density_ref, slot_hbm, stage_ref, dense_hi_ref, dense_lo_ref, pair_ref, tile_sems, slot_sems,
):
    half = BS // 2
    copies = []
    for p in range(OV * OV):
        copy = pltpu.make_async_copy(
            tile_hbm.at[jnp.maximum(pick_ref[p], 0)], stage_ref.at[p], tile_sems.at[p]
        )
        copy.start()
        copies.append(copy)
    for copy in copies:
        copy.wait()
    for q1 in range(OV):
        for q2 in range(OV):
            p = q1 * OV + q2
            tile = jnp.where(pick_ref[p] >= 0, stage_ref[p], 0.0)
            tile_hi = tile.astype(jnp.bfloat16)
            tile_lo = (tile - tile_hi.astype(jnp.float32)).astype(jnp.bfloat16)
            dense_hi_ref[q1 * BS:q1 * BS + half, q2 * BS:(q2 + 1) * BS] = tile_hi[:, :BS]
            dense_hi_ref[q1 * BS + half:(q1 + 1) * BS, q2 * BS:(q2 + 1) * BS] = tile_hi[:, BS:]
            dense_lo_ref[q1 * BS:q1 * BS + half, q2 * BS:(q2 + 1) * BS] = tile_lo[:, :BS]
            dense_lo_ref[q1 * BS + half:(q1 + 1) * BS, q2 * BS:(q2 + 1) * BS] = tile_lo[:, BS:]

    def dot(a, c, dims):
        return lax.dot_general(a, c, (dims, ((), ())), preferred_element_type=jnp.float32)

    grid_hi = hi_ref[...]
    grid_lo = lo_ref[...]
    dense_hi = dense_hi_ref[...]
    nn = ((1,), (0,))
    mixed = dot(dense_hi, grid_hi, nn) + (dot(dense_hi, grid_lo, nn) + dot(dense_lo_ref[...], grid_hi, nn))
    permuted = perm_ref[...]
    density = jnp.sum(permuted * mixed, axis=0, keepdims=True)
    potential = base_ref[...] + density - density * density * density / 6.0
    density_ref[...] = density
    weighted = permuted * (weight_ref[...] * potential)
    weighted_hi = weighted.astype(jnp.bfloat16)
    weighted_lo = (weighted - weighted_hi.astype(jnp.float32)).astype(jnp.bfloat16)
    nt = ((1,), (1,))
    terms = dot(weighted_hi, grid_hi, nt) + (dot(weighted_hi, grid_lo, nt) + dot(weighted_lo, grid_hi, nt))
    for q1 in range(OV):
        for q2 in range(OV):
            pair_ref[q1 * OV + q2, :, :BS] = terms[q1 * BS:q1 * BS + half, q2 * BS:(q2 + 1) * BS]
            pair_ref[q1 * OV + q2, :, BS:] = terms[q1 * BS + half:(q1 + 1) * BS, q2 * BS:(q2 + 1) * BS]
    pair_ref[OV * OV] = jnp.zeros(pair_ref.shape[1:], jnp.float32)

    def slot_copy(k):
        return pltpu.make_async_copy(pair_ref.at[code_ref[k]], slot_hbm.at[k], slot_sems.at[k])

    def start(k, carry):
        slot_copy(k).start()
        return carry

    def wait(k, carry):
        slot_copy(k).wait()
        return carry

    lax.fori_loop(0, slot_hbm.shape[0], start, 0)
    lax.fori_loop(0, slot_hbm.shape[0], wait, 0)


def batch_terms(source, pick, code, tables, tile_values, weights, local_pot):
    batch_count, rows, points = tables.shape
    kept_count = code.shape[0]
    span = batch_count * points
    grid_hi, grid_lo, permuted = prep_tables(source, tables)
    whole = lambda i, k, c: (0, 0)
    grid_spec = pltpu.PrefetchScalarGridSpec(
        num_scalar_prefetch=2,
        grid=(1,),
        in_specs=[
            pl.BlockSpec((rows, span), whole),
            pl.BlockSpec((rows, span), whole),
            pl.BlockSpec((rows, span), whole),
            pl.BlockSpec(memory_space=pl.ANY),
            pl.BlockSpec((1, span), whole),
            pl.BlockSpec((1, span), whole),
        ],
        out_specs=[
            pl.BlockSpec((1, span), whole),
            pl.BlockSpec(memory_space=pl.ANY),
        ],
        scratch_shapes=[
            pltpu.VMEM((OV * OV, BS // 2, 2 * BS), jnp.float32),
            pltpu.VMEM((rows, rows), jnp.bfloat16),
            pltpu.VMEM((rows, rows), jnp.bfloat16),
            pltpu.VMEM((OV * OV + 1, BS // 2, 2 * BS), jnp.float32),
            pltpu.SemaphoreType.DMA((OV * OV,)),
            pltpu.SemaphoreType.DMA((kept_count,)),
        ],
    )
    density, pair_tiles = pl.pallas_call(
        batch_kernel,
        grid_spec=grid_spec,
        out_shape=[
            jax.ShapeDtypeStruct((1, span), jnp.float32),
            jax.ShapeDtypeStruct((kept_count, BS // 2, 2 * BS), jnp.float32),
        ],
    )(
        pick,
        code,
        grid_hi,
        grid_lo,
        permuted,
        tile_values,
        weights.reshape(1, span),
        local_pot.reshape(1, span),
    )
    return density.reshape(batch_count, points), pair_tiles


def body(coeffs, occupation, kept_tiles, tile_slot, blocks, batch_slot, tables, weights, local_pot):
    devices = lax.axis_size("tiles")
    my_index = lax.axis_index("tiles")
    kept_count = kept_tiles.shape[0]
    owned_count = kept_count // devices
    batch_count = tables.shape[0]
    batch_total = batch_slot.shape[0]
    state_count = coeffs.shape[0]
    block_total = coeffs.shape[1] // BS
    points = tables.shape[-1]
    width = OV * BS

    ladder_kept = jnp.arange(kept_count, dtype=jnp.int32)
    slot_kept = jnp.zeros((kept_count,), jnp.int32).at[tile_slot].set(ladder_kept)
    pairs = kept_tiles[slot_kept]
    partial = tile_products(coeffs, occupation, pairs).reshape(devices, owned_count, BS // 2, 2 * BS)
    owned = jnp.sum(lax.all_to_all(partial, "tiles", 0, 0, tiled=False), axis=0)
    spread = jnp.broadcast_to(owned[None], (devices, owned_count, BS // 2, 2 * BS))
    tile_values = lax.all_to_all(spread, "tiles", 0, 0, tiled=False).reshape(
        kept_count, BS // 2, 2 * BS
    )

    ladder_batch = jnp.arange(batch_total, dtype=jnp.int32)
    slot_batch = jnp.zeros((batch_total,), jnp.int32).at[batch_slot].set(ladder_batch)
    my_batches = lax.dynamic_slice_in_dim(slot_batch, my_index * batch_count, batch_count)
    my_blocks = blocks[my_batches]
    canon = jnp.sort(my_blocks[0])
    ladder_ov = jnp.arange(OV, dtype=jnp.int32)
    match = my_blocks[:, :, None] == canon[None, None, :]
    source = jnp.sum(jnp.where(match, ladder_ov[None, :, None], 0), axis=1)
    row_hit = pairs[:, 0:1] == canon[None, :]
    col_hit = pairs[:, 1:2] == canon[None, :]
    present = jnp.any(row_hit, axis=1) & jnp.any(col_hit, axis=1)
    row_place = jnp.sum(jnp.where(row_hit, ladder_ov[None, :], 0), axis=1)
    col_place = jnp.sum(jnp.where(col_hit, ladder_ov[None, :], 0), axis=1)
    pair_code = row_place * OV + col_place
    ladder_pair = jnp.arange(OV * OV, dtype=jnp.int32)
    at_pair = present[None, :] & (pair_code[None, :] == ladder_pair[:, None])
    pick = jnp.where(
        jnp.any(at_pair, axis=1), jnp.sum(jnp.where(at_pair, ladder_kept[None, :], 0), axis=1), -1
    )
    code = jnp.where(present, pair_code, OV * OV)
    density, contrib = batch_terms(source, pick, code, tables, tile_values, weights, local_pot)

    terms = contrib.reshape(devices, owned_count, BS // 2, 2 * BS)
    matrix = jnp.sum(lax.all_to_all(terms, "tiles", 0, 0, tiled=False), axis=0)
    matrix = matrix.reshape(owned_count, BS * BS)
    return (density, matrix)


def solution(mesh):
    in_specs = (
        P(("groups", "tiles"), None),
        P(("groups", "tiles")),
        P("groups", None),
        P("groups"),
        P("groups", None),
        P("groups"),
        P(("groups", "tiles"), None, None),
        P(("groups", "tiles"), None),
        P(("groups", "tiles"), None),
    )
    out_specs = (P(("groups", "tiles"), None), P(("groups", "tiles"), None))
    return jax.shard_map(body, mesh=mesh, in_specs=in_specs, out_specs=out_specs, check_vma=False)
```

```python
import jax
import jax.numpy as jnp
from jax import lax
from jax.experimental import pallas as pl
from jax.experimental.pallas import tpu as pltpu
from jax.sharding import PartitionSpec as P

BS = 64
OV = 8


def tile_kernel(pairs_ref, *refs):
    group = (len(refs) - 2) // 2
    occ_ref = refs[2 * group]
    out_ref = refs[2 * group + 1]
    k = pl.program_id(0)
    occ_row = occ_ref[...]
    size = occ_row.shape[1]
    diagonal = lax.broadcasted_iota(jnp.int32, (size, size), 0) == lax.broadcasted_iota(jnp.int32, (size, size), 1)
    occ = jnp.sum(jnp.where(diagonal, occ_row, 0.0), axis=1, keepdims=True)
    for i in range(group):
        row_block = pairs_ref[2 * (group * k + i)]
        col_block = pairs_ref[2 * (group * k + i) + 1]
        left = refs[i][...]
        right = refs[group + i][...] * occ
        left = jnp.where(row_block % 2 == 0, left[:, :BS], left[:, BS:])
        right = jnp.where(col_block % 2 == 0, right[:, :BS], right[:, BS:])
        out_ref[i] = lax.dot_general(
            left,
            right,
            (((0,), (0,)), ((), ())),
            precision=lax.Precision.HIGHEST,
            preferred_element_type=jnp.float32,
        )


def tile_products(coeffs, occupation, pairs):
    state_count = coeffs.shape[0]
    kept_count = pairs.shape[0]
    group = next(g for g in (16, 8, 4, 2, 1) if kept_count % g == 0)

    def block_of(i, side):
        return pl.BlockSpec(
            (state_count, 2 * BS), lambda k, p: (0, p[2 * (group * k + i) + side] // 2)
        )

    grid_spec = pltpu.PrefetchScalarGridSpec(
        num_scalar_prefetch=1,
        grid=(kept_count // group,),
        in_specs=[block_of(i, 0) for i in range(group)]
        + [block_of(i, 1) for i in range(group)]
        + [pl.BlockSpec((1, state_count), lambda k, p: (0, 0))],
        out_specs=pl.BlockSpec((group, BS, BS), lambda k, p: (k, 0, 0)),
    )
    return pl.pallas_call(
        tile_kernel,
        grid_spec=grid_spec,
        out_shape=jax.ShapeDtypeStruct((kept_count, BS, BS), jnp.float32),
    )(pairs.reshape(-1), *([coeffs] * (2 * group)), occupation.reshape(1, state_count))


def split_dot(left, right, dims):
    left_hi = left.astype(jnp.bfloat16)
    left_lo = (left - left_hi.astype(jnp.float32)).astype(jnp.bfloat16)
    right_hi = right.astype(jnp.bfloat16)
    right_lo = (right - right_hi.astype(jnp.float32)).astype(jnp.bfloat16)

    def one(a, b):
        return lax.dot_general(a, b, (dims, ((), ())), preferred_element_type=jnp.float32)

    return one(left_hi, right_hi) + (one(left_hi, right_lo) + one(left_lo, right_hi))


def prep_kernel(source_ref, table_hbm, hi_ref, lo_ref, perm_ref, canon_ref, chunk_ref, table_sems, chunk_sems):
    half = BS // 2
    lane = 2 * BS
    batch_count, _, points = table_hbm.shape
    copies = []
    chunk_copies = []
    for b in range(batch_count):
        for q in range(OV):
            start = pl.multiple_of(source_ref[b * OV + q] * BS, BS)
            copy = pltpu.make_async_copy(
                table_hbm.at[b, pl.ds(start, BS), :],
                canon_ref.at[q * BS:(q + 1) * BS, b * points:(b + 1) * points],
                table_sems.at[b * OV + q],
            )
            copy.start()
            copies.append(copy)
            for h in range(points // lane):
                c = b * (points // lane) + h
                copy = pltpu.make_async_copy(
                    table_hbm.at[b, pl.ds(start, BS), h * lane:(h + 1) * lane],
                    chunk_ref.at[c, q * BS:(q + 1) * BS, :],
                    chunk_sems.at[c * OV + q],
                )
                copy.start()
                chunk_copies.append(copy)
    for copy in copies:
        copy.wait()
    grid = canon_ref[...]
    grid_hi = grid.astype(jnp.bfloat16)
    hi_ref[...] = grid_hi
    lo_ref[...] = (grid - grid_hi.astype(jnp.float32)).astype(jnp.bfloat16)
    for copy in chunk_copies:
        copy.wait()
    for c in range(chunk_ref.shape[0]):
        for q in range(OV):
            perm_ref[q * BS:q * BS + half, c * lane:(c + 1) * lane] = chunk_ref[c, pl.ds(q * BS, half, stride=2), :]
            perm_ref[q * BS + half:(q + 1) * BS, c * lane:(c + 1) * lane] = chunk_ref[
                c, pl.ds(q * BS + 1, half, stride=2), :
            ]


def prep_tables(source, tables):
    batch_count, rows, points = tables.shape
    span = batch_count * points
    whole = lambda i, s: (0, 0)
    grid_spec = pltpu.PrefetchScalarGridSpec(
        num_scalar_prefetch=1,
        grid=(1,),
        in_specs=[pl.BlockSpec(memory_space=pl.ANY)],
        out_specs=[
            pl.BlockSpec((rows, span), whole),
            pl.BlockSpec((rows, span), whole),
            pl.BlockSpec((rows, span), whole),
        ],
        scratch_shapes=[
            pltpu.VMEM((rows, span), jnp.float32),
            pltpu.VMEM((span // (2 * BS), rows, 2 * BS), jnp.float32),
            pltpu.SemaphoreType.DMA((batch_count * OV,)),
            pltpu.SemaphoreType.DMA((span // (2 * BS) * OV,)),
        ],
    )
    return pl.pallas_call(
        prep_kernel,
        grid_spec=grid_spec,
        out_shape=[
            jax.ShapeDtypeStruct((rows, span), jnp.bfloat16),
            jax.ShapeDtypeStruct((rows, span), jnp.bfloat16),
            jax.ShapeDtypeStruct((rows, span), jnp.float32),
        ],
    )(source.reshape(-1), tables)


def batch_kernel(
    pick_ref, hi_ref, lo_ref, perm_ref, tile_hbm, weight_ref, base_ref,
    density_ref, pair_ref, stage_ref, dense_hi_ref, dense_lo_ref, tile_sems,
):
    half = BS // 2
    copies = []
    for p in range(OV * OV):
        copy = pltpu.make_async_copy(
            tile_hbm.at[jnp.maximum(pick_ref[p], 0)], stage_ref.at[p], tile_sems.at[p]
        )
        copy.start()
        copies.append(copy)
    for copy in copies:
        copy.wait()
    for q1 in range(OV):
        for q2 in range(OV):
            p = q1 * OV + q2
            tile = jnp.where(pick_ref[p] >= 0, stage_ref[p], 0.0)
            tile_hi = tile.astype(jnp.bfloat16)
            tile_lo = (tile - tile_hi.astype(jnp.float32)).astype(jnp.bfloat16)
            dense_hi_ref[q1 * BS:q1 * BS + half, q2 * BS:(q2 + 1) * BS] = tile_hi[:, :BS]
            dense_hi_ref[q1 * BS + half:(q1 + 1) * BS, q2 * BS:(q2 + 1) * BS] = tile_hi[:, BS:]
            dense_lo_ref[q1 * BS:q1 * BS + half, q2 * BS:(q2 + 1) * BS] = tile_lo[:, :BS]
            dense_lo_ref[q1 * BS + half:(q1 + 1) * BS, q2 * BS:(q2 + 1) * BS] = tile_lo[:, BS:]

    def dot(a, c, dims):
        return lax.dot_general(a, c, (dims, ((), ())), preferred_element_type=jnp.float32)

    grid_hi = hi_ref[...]
    grid_lo = lo_ref[...]
    dense_hi = dense_hi_ref[...]
    nn = ((1,), (0,))
    mixed = dot(dense_hi, grid_hi, nn) + (dot(dense_hi, grid_lo, nn) + dot(dense_lo_ref[...], grid_hi, nn))
    permuted = perm_ref[...]
    density = jnp.sum(permuted * mixed, axis=0, keepdims=True)
    potential = base_ref[...] + density - density * density * density / 6.0
    density_ref[...] = density
    weighted = permuted * (weight_ref[...] * potential)
    weighted_hi = weighted.astype(jnp.bfloat16)
    weighted_lo = (weighted - weighted_hi.astype(jnp.float32)).astype(jnp.bfloat16)
    nt = ((1,), (1,))
    terms = dot(weighted_hi, grid_hi, nt) + (dot(weighted_hi, grid_lo, nt) + dot(weighted_lo, grid_hi, nt))
    for q1 in range(OV):
        for q2 in range(OV):
            pair_ref[q1 * OV + q2, :, :BS] = terms[q1 * BS:q1 * BS + half, q2 * BS:(q2 + 1) * BS]
            pair_ref[q1 * OV + q2, :, BS:] = terms[q1 * BS + half:(q1 + 1) * BS, q2 * BS:(q2 + 1) * BS]


def batch_terms(source, pick, tables, tile_values, weights, local_pot):
    batch_count, rows, points = tables.shape
    span = batch_count * points
    grid_hi, grid_lo, permuted = prep_tables(source, tables)
    whole = lambda i, k: (0, 0)
    grid_spec = pltpu.PrefetchScalarGridSpec(
        num_scalar_prefetch=1,
        grid=(1,),
        in_specs=[
            pl.BlockSpec((rows, span), whole),
            pl.BlockSpec((rows, span), whole),
            pl.BlockSpec((rows, span), whole),
            pl.BlockSpec(memory_space=pl.ANY),
            pl.BlockSpec((1, span), whole),
            pl.BlockSpec((1, span), whole),
        ],
        out_specs=[
            pl.BlockSpec((1, span), whole),
            pl.BlockSpec((OV * OV, BS // 2, 2 * BS), lambda i, k: (0, 0, 0)),
        ],
        scratch_shapes=[
            pltpu.VMEM((OV * OV, BS // 2, 2 * BS), jnp.float32),
            pltpu.VMEM((rows, rows), jnp.bfloat16),
            pltpu.VMEM((rows, rows), jnp.bfloat16),
            pltpu.SemaphoreType.DMA((OV * OV,)),
        ],
    )
    density, pair_tiles = pl.pallas_call(
        batch_kernel,
        grid_spec=grid_spec,
        out_shape=[
            jax.ShapeDtypeStruct((1, span), jnp.float32),
            jax.ShapeDtypeStruct((OV * OV, BS // 2, 2 * BS), jnp.float32),
        ],
    )(
        pick,
        grid_hi,
        grid_lo,
        permuted,
        tile_values,
        weights.reshape(1, span),
        local_pot.reshape(1, span),
    )
    return density.reshape(batch_count, points), pair_tiles


def body(coeffs, occupation, kept_tiles, tile_slot, blocks, batch_slot, tables, weights, local_pot):
    devices = lax.axis_size("tiles")
    my_index = lax.axis_index("tiles")
    kept_count = kept_tiles.shape[0]
    owned_count = kept_count // devices
    batch_count = tables.shape[0]
    batch_total = batch_slot.shape[0]
    state_count = coeffs.shape[0]
    block_total = coeffs.shape[1] // BS
    points = tables.shape[-1]
    width = OV * BS

    ladder_kept = jnp.arange(kept_count, dtype=jnp.int32)
    slot_kept = jnp.zeros((kept_count,), jnp.int32).at[tile_slot].set(ladder_kept)
    pairs = kept_tiles[slot_kept]
    partial = tile_products(coeffs, occupation, pairs).reshape(devices, owned_count, BS // 2, 2 * BS)
    owned = jnp.sum(lax.all_to_all(partial, "tiles", 0, 0, tiled=False), axis=0)
    spread = jnp.broadcast_to(owned[None], (devices, owned_count, BS // 2, 2 * BS))
    tile_values = lax.all_to_all(spread, "tiles", 0, 0, tiled=False).reshape(
        kept_count, BS // 2, 2 * BS
    )

    ladder_batch = jnp.arange(batch_total, dtype=jnp.int32)
    slot_batch = jnp.zeros((batch_total,), jnp.int32).at[batch_slot].set(ladder_batch)
    my_batches = lax.dynamic_slice_in_dim(slot_batch, my_index * batch_count, batch_count)
    my_blocks = blocks[my_batches]
    canon = jnp.sort(my_blocks[0])
    ladder_ov = jnp.arange(OV, dtype=jnp.int32)
    match = my_blocks[:, :, None] == canon[None, None, :]
    source = jnp.sum(jnp.where(match, ladder_ov[None, :, None], 0), axis=1)
    row_hit = pairs[:, 0:1] == canon[None, :]
    col_hit = pairs[:, 1:2] == canon[None, :]
    present = jnp.any(row_hit, axis=1) & jnp.any(col_hit, axis=1)
    row_place = jnp.sum(jnp.where(row_hit, ladder_ov[None, :], 0), axis=1)
    col_place = jnp.sum(jnp.where(col_hit, ladder_ov[None, :], 0), axis=1)
    pair_code = row_place * OV + col_place
    ladder_pair = jnp.arange(OV * OV, dtype=jnp.int32)
    at_pair = present[None, :] & (pair_code[None, :] == ladder_pair[:, None])
    pick = jnp.where(
        jnp.any(at_pair, axis=1), jnp.sum(jnp.where(at_pair, ladder_kept[None, :], 0), axis=1), -1
    )
    density, pair_tiles = batch_terms(source, pick, tables, tile_values, weights, local_pot)
    contrib = jnp.where(present[:, None, None], pair_tiles[pair_code], 0.0)

    terms = contrib.reshape(devices, owned_count, BS // 2, 2 * BS)
    matrix = jnp.sum(lax.all_to_all(terms, "tiles", 0, 0, tiled=False), axis=0)
    matrix = matrix.reshape(owned_count, BS * BS)
    return (density, matrix)


def solution(mesh):
    in_specs = (
        P(("groups", "tiles"), None),
        P(("groups", "tiles")),
        P("groups", None),
        P("groups"),
        P("groups", None),
        P("groups"),
        P(("groups", "tiles"), None, None),
        P(("groups", "tiles"), None),
        P(("groups", "tiles"), None),
    )
    out_specs = (P(("groups", "tiles"), None), P(("groups", "tiles"), None))
    return jax.shard_map(body, mesh=mesh, in_specs=in_specs, out_specs=out_specs, check_vma=False)
```

```python
import jax
import jax.numpy as jnp
from jax import lax
from jax.experimental import pallas as pl
from jax.experimental.pallas import tpu as pltpu
from jax.sharding import PartitionSpec as P

BS = 64
OV = 8


def tile_kernel(pairs_ref, *refs):
    group = (len(refs) - 2) // 2
    occ_ref = refs[2 * group]
    out_ref = refs[2 * group + 1]
    k = pl.program_id(0)
    occ_row = occ_ref[...]
    size = occ_row.shape[1]
    diagonal = lax.broadcasted_iota(jnp.int32, (size, size), 0) == lax.broadcasted_iota(jnp.int32, (size, size), 1)
    occ = jnp.sum(jnp.where(diagonal, occ_row, 0.0), axis=1, keepdims=True)
    for i in range(group):
        row_block = pairs_ref[2 * (group * k + i)]
        col_block = pairs_ref[2 * (group * k + i) + 1]
        left = refs[i][...]
        right = refs[group + i][...] * occ
        left = jnp.where(row_block % 2 == 0, left[:, :BS], left[:, BS:])
        right = jnp.where(col_block % 2 == 0, right[:, :BS], right[:, BS:])
        out_ref[i] = lax.dot_general(
            left,
            right,
            (((0,), (0,)), ((), ())),
            precision=lax.Precision.HIGHEST,
            preferred_element_type=jnp.float32,
        )


def tile_products(coeffs, occupation, pairs):
    state_count = coeffs.shape[0]
    kept_count = pairs.shape[0]
    group = next(g for g in (16, 8, 4, 2, 1) if kept_count % g == 0)

    def block_of(i, side):
        return pl.BlockSpec(
            (state_count, 2 * BS), lambda k, p: (0, p[2 * (group * k + i) + side] // 2)
        )

    grid_spec = pltpu.PrefetchScalarGridSpec(
        num_scalar_prefetch=1,
        grid=(kept_count // group,),
        in_specs=[block_of(i, 0) for i in range(group)]
        + [block_of(i, 1) for i in range(group)]
        + [pl.BlockSpec((1, state_count), lambda k, p: (0, 0))],
        out_specs=pl.BlockSpec((group, BS, BS), lambda k, p: (k, 0, 0)),
    )
    return pl.pallas_call(
        tile_kernel,
        grid_spec=grid_spec,
        out_shape=jax.ShapeDtypeStruct((kept_count, BS, BS), jnp.float32),
    )(pairs.reshape(-1), *([coeffs] * (2 * group)), occupation.reshape(1, state_count))


def split_dot(left, right, dims):
    left_hi = left.astype(jnp.bfloat16)
    left_lo = (left - left_hi.astype(jnp.float32)).astype(jnp.bfloat16)
    right_hi = right.astype(jnp.bfloat16)
    right_lo = (right - right_hi.astype(jnp.float32)).astype(jnp.bfloat16)

    def one(a, b):
        return lax.dot_general(a, b, (dims, ((), ())), preferred_element_type=jnp.float32)

    return one(left_hi, right_hi) + (one(left_hi, right_lo) + one(left_lo, right_hi))


def prep_kernel(source_ref, table_hbm, hi_ref, lo_ref, perm_ref, canon_ref, chunk_ref, table_sems, chunk_sems):
    half = BS // 2
    lane = 2 * BS
    batch_count, _, points = table_hbm.shape
    copies = []
    chunk_copies = []
    for b in range(batch_count):
        for q in range(OV):
            start = pl.multiple_of(source_ref[b * OV + q] * BS, BS)
            copy = pltpu.make_async_copy(
                table_hbm.at[b, pl.ds(start, BS), :],
                canon_ref.at[q * BS:(q + 1) * BS, b * points:(b + 1) * points],
                table_sems.at[b * OV + q],
            )
            copy.start()
            copies.append(copy)
            for h in range(points // lane):
                c = b * (points // lane) + h
                copy = pltpu.make_async_copy(
                    table_hbm.at[b, pl.ds(start, BS), h * lane:(h + 1) * lane],
                    chunk_ref.at[c, q * BS:(q + 1) * BS, :],
                    chunk_sems.at[c * OV + q],
                )
                copy.start()
                chunk_copies.append(copy)
    for copy in copies:
        copy.wait()
    grid = canon_ref[...]
    grid_hi = grid.astype(jnp.bfloat16)
    hi_ref[...] = grid_hi
    lo_ref[...] = (grid - grid_hi.astype(jnp.float32)).astype(jnp.bfloat16)
    for copy in chunk_copies:
        copy.wait()
    for c in range(chunk_ref.shape[0]):
        for q in range(OV):
            perm_ref[q * BS:q * BS + half, c * lane:(c + 1) * lane] = chunk_ref[c, pl.ds(q * BS, half, stride=2), :]
            perm_ref[q * BS + half:(q + 1) * BS, c * lane:(c + 1) * lane] = chunk_ref[
                c, pl.ds(q * BS + 1, half, stride=2), :
            ]


def prep_tables(source, tables):
    batch_count, rows, points = tables.shape
    span = batch_count * points
    whole = lambda i, s: (0, 0)
    grid_spec = pltpu.PrefetchScalarGridSpec(
        num_scalar_prefetch=1,
        grid=(1,),
        in_specs=[pl.BlockSpec(memory_space=pl.ANY)],
        out_specs=[
            pl.BlockSpec((rows, span), whole),
            pl.BlockSpec((rows, span), whole),
            pl.BlockSpec((rows, span), whole),
        ],
        scratch_shapes=[
            pltpu.VMEM((rows, span), jnp.float32),
            pltpu.VMEM((span // (2 * BS), rows, 2 * BS), jnp.float32),
            pltpu.SemaphoreType.DMA((batch_count * OV,)),
            pltpu.SemaphoreType.DMA((span // (2 * BS) * OV,)),
        ],
    )
    return pl.pallas_call(
        prep_kernel,
        grid_spec=grid_spec,
        out_shape=[
            jax.ShapeDtypeStruct((rows, span), jnp.bfloat16),
            jax.ShapeDtypeStruct((rows, span), jnp.bfloat16),
            jax.ShapeDtypeStruct((rows, span), jnp.float32),
        ],
    )(source.reshape(-1), tables)


def batch_kernel(
    pick_ref, hi_ref, lo_ref, perm_hbm, tile_hbm, weight_ref, base_ref,
    density_ref, pair_ref, stage_ref, dense_hi_ref, dense_lo_ref, perm_ref, tile_sems, perm_sem,
):
    half = BS // 2
    perm_copy = pltpu.make_async_copy(perm_hbm, perm_ref, perm_sem.at[0])
    perm_copy.start()
    copies = []
    for p in range(OV * OV):
        copy = pltpu.make_async_copy(
            tile_hbm.at[jnp.maximum(pick_ref[p], 0)], stage_ref.at[p], tile_sems.at[p]
        )
        copy.start()
        copies.append(copy)
    for copy in copies:
        copy.wait()
    for q1 in range(OV):
        for q2 in range(OV):
            p = q1 * OV + q2
            tile = jnp.where(pick_ref[p] >= 0, stage_ref[p], 0.0)
            tile_hi = tile.astype(jnp.bfloat16)
            tile_lo = (tile - tile_hi.astype(jnp.float32)).astype(jnp.bfloat16)
            dense_hi_ref[q1 * BS:q1 * BS + half, q2 * BS:(q2 + 1) * BS] = tile_hi[:, :BS]
            dense_hi_ref[q1 * BS + half:(q1 + 1) * BS, q2 * BS:(q2 + 1) * BS] = tile_hi[:, BS:]
            dense_lo_ref[q1 * BS:q1 * BS + half, q2 * BS:(q2 + 1) * BS] = tile_lo[:, :BS]
            dense_lo_ref[q1 * BS + half:(q1 + 1) * BS, q2 * BS:(q2 + 1) * BS] = tile_lo[:, BS:]

    def dot(a, c, dims):
        return lax.dot_general(a, c, (dims, ((), ())), preferred_element_type=jnp.float32)

    grid_hi = hi_ref[...]
    grid_lo = lo_ref[...]
    dense_hi = dense_hi_ref[...]
    nn = ((1,), (0,))
    mixed = dot(dense_hi, grid_hi, nn) + (dot(dense_hi, grid_lo, nn) + dot(dense_lo_ref[...], grid_hi, nn))
    perm_copy.wait()
    permuted = perm_ref[...]
    density = jnp.sum(permuted * mixed, axis=0, keepdims=True)
    potential = base_ref[...] + density - density * density * density / 6.0
    density_ref[...] = density
    weighted = permuted * (weight_ref[...] * potential)
    weighted_hi = weighted.astype(jnp.bfloat16)
    weighted_lo = (weighted - weighted_hi.astype(jnp.float32)).astype(jnp.bfloat16)
    nt = ((1,), (1,))
    terms = dot(weighted_hi, grid_hi, nt) + (dot(weighted_hi, grid_lo, nt) + dot(weighted_lo, grid_hi, nt))
    for q1 in range(OV):
        for q2 in range(OV):
            pair_ref[q1 * OV + q2, :, :BS] = terms[q1 * BS:q1 * BS + half, q2 * BS:(q2 + 1) * BS]
            pair_ref[q1 * OV + q2, :, BS:] = terms[q1 * BS + half:(q1 + 1) * BS, q2 * BS:(q2 + 1) * BS]


def batch_terms(source, pick, tables, tile_values, weights, local_pot):
    batch_count, rows, points = tables.shape
    span = batch_count * points
    grid_hi, grid_lo, permuted = prep_tables(source, tables)
    whole = lambda i, k: (0, 0)
    grid_spec = pltpu.PrefetchScalarGridSpec(
        num_scalar_prefetch=1,
        grid=(1,),
        in_specs=[
            pl.BlockSpec((rows, span), whole),
            pl.BlockSpec((rows, span), whole),
            pl.BlockSpec(memory_space=pl.ANY),
            pl.BlockSpec(memory_space=pl.ANY),
            pl.BlockSpec((1, span), whole),
            pl.BlockSpec((1, span), whole),
        ],
        out_specs=[
            pl.BlockSpec((1, span), whole),
            pl.BlockSpec((OV * OV, BS // 2, 2 * BS), lambda i, k: (0, 0, 0)),
        ],
        scratch_shapes=[
            pltpu.VMEM((OV * OV, BS // 2, 2 * BS), jnp.float32),
            pltpu.VMEM((rows, rows), jnp.bfloat16),
            pltpu.VMEM((rows, rows), jnp.bfloat16),
            pltpu.VMEM((rows, span), jnp.float32),
            pltpu.SemaphoreType.DMA((OV * OV,)),
            pltpu.SemaphoreType.DMA((1,)),
        ],
    )
    density, pair_tiles = pl.pallas_call(
        batch_kernel,
        grid_spec=grid_spec,
        out_shape=[
            jax.ShapeDtypeStruct((1, span), jnp.float32),
            jax.ShapeDtypeStruct((OV * OV, BS // 2, 2 * BS), jnp.float32),
        ],
    )(
        pick,
        grid_hi,
        grid_lo,
        permuted,
        tile_values,
        weights.reshape(1, span),
        local_pot.reshape(1, span),
    )
    return density.reshape(batch_count, points), pair_tiles


def body(coeffs, occupation, kept_tiles, tile_slot, blocks, batch_slot, tables, weights, local_pot):
    devices = lax.axis_size("tiles")
    my_index = lax.axis_index("tiles")
    kept_count = kept_tiles.shape[0]
    owned_count = kept_count // devices
    batch_count = tables.shape[0]
    batch_total = batch_slot.shape[0]
    state_count = coeffs.shape[0]
    block_total = coeffs.shape[1] // BS
    points = tables.shape[-1]
    width = OV * BS

    ladder_kept = jnp.arange(kept_count, dtype=jnp.int32)
    slot_kept = jnp.zeros((kept_count,), jnp.int32).at[tile_slot].set(ladder_kept)
    pairs = kept_tiles[slot_kept]
    partial = tile_products(coeffs, occupation, pairs).reshape(devices, owned_count, BS // 2, 2 * BS)
    owned = jnp.sum(lax.all_to_all(partial, "tiles", 0, 0, tiled=False), axis=0)
    spread = jnp.broadcast_to(owned[None], (devices, owned_count, BS // 2, 2 * BS))
    tile_values = lax.all_to_all(spread, "tiles", 0, 0, tiled=False).reshape(
        kept_count, BS // 2, 2 * BS
    )

    ladder_batch = jnp.arange(batch_total, dtype=jnp.int32)
    slot_batch = jnp.zeros((batch_total,), jnp.int32).at[batch_slot].set(ladder_batch)
    my_batches = lax.dynamic_slice_in_dim(slot_batch, my_index * batch_count, batch_count)
    my_blocks = blocks[my_batches]
    canon = jnp.sort(my_blocks[0])
    ladder_ov = jnp.arange(OV, dtype=jnp.int32)
    match = my_blocks[:, :, None] == canon[None, None, :]
    source = jnp.sum(jnp.where(match, ladder_ov[None, :, None], 0), axis=1)
    row_hit = pairs[:, 0:1] == canon[None, :]
    col_hit = pairs[:, 1:2] == canon[None, :]
    present = jnp.any(row_hit, axis=1) & jnp.any(col_hit, axis=1)
    row_place = jnp.sum(jnp.where(row_hit, ladder_ov[None, :], 0), axis=1)
    col_place = jnp.sum(jnp.where(col_hit, ladder_ov[None, :], 0), axis=1)
    pair_code = row_place * OV + col_place
    ladder_pair = jnp.arange(OV * OV, dtype=jnp.int32)
    at_pair = present[None, :] & (pair_code[None, :] == ladder_pair[:, None])
    pick = jnp.where(
        jnp.any(at_pair, axis=1), jnp.sum(jnp.where(at_pair, ladder_kept[None, :], 0), axis=1), -1
    )
    density, pair_tiles = batch_terms(source, pick, tables, tile_values, weights, local_pot)
    contrib = jnp.where(present[:, None, None], pair_tiles[pair_code], 0.0)

    terms = contrib.reshape(devices, owned_count, BS // 2, 2 * BS)
    matrix = jnp.sum(lax.all_to_all(terms, "tiles", 0, 0, tiled=False), axis=0)
    matrix = matrix.reshape(owned_count, BS * BS)
    return (density, matrix)


def solution(mesh):
    in_specs = (
        P(("groups", "tiles"), None),
        P(("groups", "tiles")),
        P("groups", None),
        P("groups"),
        P("groups", None),
        P("groups"),
        P(("groups", "tiles"), None, None),
        P(("groups", "tiles"), None),
        P(("groups", "tiles"), None),
    )
    out_specs = (P(("groups", "tiles"), None), P(("groups", "tiles"), None))
    return jax.shard_map(body, mesh=mesh, in_specs=in_specs, out_specs=out_specs, check_vma=False)
```

```python
import jax
import jax.numpy as jnp
from jax import lax
from jax.experimental import pallas as pl
from jax.experimental.pallas import tpu as pltpu
from jax.sharding import PartitionSpec as P

BS = 64
OV = 8


def tile_kernel(pairs_ref, *refs):
    group = (len(refs) - 2) // 2
    occ_ref = refs[2 * group]
    out_ref = refs[2 * group + 1]
    k = pl.program_id(0)
    occ_row = occ_ref[...]
    size = occ_row.shape[1]
    diagonal = lax.broadcasted_iota(jnp.int32, (size, size), 0) == lax.broadcasted_iota(jnp.int32, (size, size), 1)
    occ = jnp.sum(jnp.where(diagonal, occ_row, 0.0), axis=1, keepdims=True)
    for i in range(group):
        row_block = pairs_ref[2 * (group * k + i)]
        col_block = pairs_ref[2 * (group * k + i) + 1]
        left = refs[i][...]
        right = refs[group + i][...] * occ
        left = jnp.where(row_block % 2 == 0, left[:, :BS], left[:, BS:])
        right = jnp.where(col_block % 2 == 0, right[:, :BS], right[:, BS:])
        out_ref[i] = lax.dot_general(
            left,
            right,
            (((0,), (0,)), ((), ())),
            precision=lax.Precision.HIGHEST,
            preferred_element_type=jnp.float32,
        )


def tile_products(coeffs, occupation, pairs):
    state_count = coeffs.shape[0]
    kept_count = pairs.shape[0]
    group = next(g for g in (16, 8, 4, 2, 1) if kept_count % g == 0)

    def block_of(i, side):
        return pl.BlockSpec(
            (state_count, 2 * BS), lambda k, p: (0, p[2 * (group * k + i) + side] // 2)
        )

    grid_spec = pltpu.PrefetchScalarGridSpec(
        num_scalar_prefetch=1,
        grid=(kept_count // group,),
        in_specs=[block_of(i, 0) for i in range(group)]
        + [block_of(i, 1) for i in range(group)]
        + [pl.BlockSpec((1, state_count), lambda k, p: (0, 0))],
        out_specs=pl.BlockSpec((group, BS, BS), lambda k, p: (k, 0, 0)),
    )
    return pl.pallas_call(
        tile_kernel,
        grid_spec=grid_spec,
        out_shape=jax.ShapeDtypeStruct((kept_count, BS, BS), jnp.float32),
    )(pairs.reshape(-1), *([coeffs] * (2 * group)), occupation.reshape(1, state_count))


def split_dot(left, right, dims):
    left_hi = left.astype(jnp.bfloat16)
    left_lo = (left - left_hi.astype(jnp.float32)).astype(jnp.bfloat16)
    right_hi = right.astype(jnp.bfloat16)
    right_lo = (right - right_hi.astype(jnp.float32)).astype(jnp.bfloat16)

    def one(a, b):
        return lax.dot_general(a, b, (dims, ((), ())), preferred_element_type=jnp.float32)

    return one(left_hi, right_hi) + (one(left_hi, right_lo) + one(left_lo, right_hi))


def prep_kernel(source_ref, table_hbm, hi_ref, lo_ref, perm_ref, canon_ref, chunk_ref, table_sems, chunk_sems):
    half = BS // 2
    lane = 2 * BS
    batch_count, _, points = table_hbm.shape
    copies = []
    chunk_copies = []
    for b in range(batch_count):
        for q in range(OV):
            start = pl.multiple_of(source_ref[b * OV + q] * BS, BS)
            copy = pltpu.make_async_copy(
                table_hbm.at[b, pl.ds(start, BS), :],
                canon_ref.at[q * BS:(q + 1) * BS, b * points:(b + 1) * points],
                table_sems.at[b * OV + q],
            )
            copy.start()
            copies.append(copy)
            for h in range(points // lane):
                c = b * (points // lane) + h
                copy = pltpu.make_async_copy(
                    table_hbm.at[b, pl.ds(start, BS), h * lane:(h + 1) * lane],
                    chunk_ref.at[c, q * BS:(q + 1) * BS, :],
                    chunk_sems.at[c * OV + q],
                )
                copy.start()
                chunk_copies.append(copy)
    for copy in copies:
        copy.wait()
    grid = canon_ref[...]
    grid_hi = grid.astype(jnp.bfloat16)
    hi_ref[...] = grid_hi
    lo_ref[...] = (grid - grid_hi.astype(jnp.float32)).astype(jnp.bfloat16)
    for copy in chunk_copies:
        copy.wait()
    for c in range(chunk_ref.shape[0]):
        for q in range(OV):
            perm_ref[q * BS:q * BS + half, c * lane:(c + 1) * lane] = chunk_ref[c, pl.ds(q * BS, half, stride=2), :]
            perm_ref[q * BS + half:(q + 1) * BS, c * lane:(c + 1) * lane] = chunk_ref[
                c, pl.ds(q * BS + 1, half, stride=2), :
            ]


def prep_tables(source, tables):
    batch_count, rows, points = tables.shape
    span = batch_count * points
    whole = lambda i, s: (0, 0)
    grid_spec = pltpu.PrefetchScalarGridSpec(
        num_scalar_prefetch=1,
        grid=(1,),
        in_specs=[pl.BlockSpec(memory_space=pl.ANY)],
        out_specs=[
            pl.BlockSpec((rows, span), whole),
            pl.BlockSpec((rows, span), whole),
            pl.BlockSpec((rows, span), whole),
        ],
        scratch_shapes=[
            pltpu.VMEM((rows, span), jnp.float32),
            pltpu.VMEM((span // (2 * BS), rows, 2 * BS), jnp.float32),
            pltpu.SemaphoreType.DMA((batch_count * OV,)),
            pltpu.SemaphoreType.DMA((span // (2 * BS) * OV,)),
        ],
    )
    return pl.pallas_call(
        prep_kernel,
        grid_spec=grid_spec,
        out_shape=[
            jax.ShapeDtypeStruct((rows, span), jnp.bfloat16),
            jax.ShapeDtypeStruct((rows, span), jnp.bfloat16),
            jax.ShapeDtypeStruct((rows, span), jnp.float32),
        ],
    )(source.reshape(-1), tables)


def batch_kernel(
    pick_ref, code_ref, hi_ref, lo_ref, perm_ref, tile_hbm, weight_ref, base_ref,
    density_ref, slot_ref, stage_ref, dense_hi_ref, dense_lo_ref, pair_ref, tile_sems,
):
    half = BS // 2
    copies = []
    for p in range(OV * OV):
        copy = pltpu.make_async_copy(
            tile_hbm.at[jnp.maximum(pick_ref[p], 0)], stage_ref.at[p], tile_sems.at[p]
        )
        copy.start()
        copies.append(copy)
    for copy in copies:
        copy.wait()
    for q1 in range(OV):
        for q2 in range(OV):
            p = q1 * OV + q2
            tile = jnp.where(pick_ref[p] >= 0, stage_ref[p], 0.0)
            tile_hi = tile.astype(jnp.bfloat16)
            tile_lo = (tile - tile_hi.astype(jnp.float32)).astype(jnp.bfloat16)
            dense_hi_ref[q1 * BS:q1 * BS + half, q2 * BS:(q2 + 1) * BS] = tile_hi[:, :BS]
            dense_hi_ref[q1 * BS + half:(q1 + 1) * BS, q2 * BS:(q2 + 1) * BS] = tile_hi[:, BS:]
            dense_lo_ref[q1 * BS:q1 * BS + half, q2 * BS:(q2 + 1) * BS] = tile_lo[:, :BS]
            dense_lo_ref[q1 * BS + half:(q1 + 1) * BS, q2 * BS:(q2 + 1) * BS] = tile_lo[:, BS:]

    def dot(a, c, dims):
        return lax.dot_general(a, c, (dims, ((), ())), preferred_element_type=jnp.float32)

    grid_hi = hi_ref[...]
    grid_lo = lo_ref[...]
    dense_hi = dense_hi_ref[...]
    nn = ((1,), (0,))
    mixed = dot(dense_hi, grid_hi, nn) + (dot(dense_hi, grid_lo, nn) + dot(dense_lo_ref[...], grid_hi, nn))
    permuted = perm_ref[...]
    density = jnp.sum(permuted * mixed, axis=0, keepdims=True)
    potential = base_ref[...] + density - density * density * density / 6.0
    density_ref[...] = density
    weighted = permuted * (weight_ref[...] * potential)
    weighted_hi = weighted.astype(jnp.bfloat16)
    weighted_lo = (weighted - weighted_hi.astype(jnp.float32)).astype(jnp.bfloat16)
    nt = ((1,), (1,))
    terms = dot(weighted_hi, grid_hi, nt) + (dot(weighted_hi, grid_lo, nt) + dot(weighted_lo, grid_hi, nt))
    for q1 in range(OV):
        for q2 in range(OV):
            pair_ref[q1 * OV + q2, :, :BS] = terms[q1 * BS:q1 * BS + half, q2 * BS:(q2 + 1) * BS]
            pair_ref[q1 * OV + q2, :, BS:] = terms[q1 * BS + half:(q1 + 1) * BS, q2 * BS:(q2 + 1) * BS]
    pair_ref[OV * OV] = jnp.zeros(pair_ref.shape[1:], jnp.float32)

    def place(k, carry):
        slot_ref[k] = pair_ref[code_ref[k]]
        return carry

    lax.fori_loop(0, slot_ref.shape[0], place, 0)


def batch_terms(source, pick, code, tables, tile_values, weights, local_pot):
    batch_count, rows, points = tables.shape
    kept_count = code.shape[0]
    span = batch_count * points
    grid_hi, grid_lo, permuted = prep_tables(source, tables)
    whole = lambda i, k, c: (0, 0)
    grid_spec = pltpu.PrefetchScalarGridSpec(
        num_scalar_prefetch=2,
        grid=(1,),
        in_specs=[
            pl.BlockSpec((rows, span), whole),
            pl.BlockSpec((rows, span), whole),
            pl.BlockSpec((rows, span), whole),
            pl.BlockSpec(memory_space=pl.ANY),
            pl.BlockSpec((1, span), whole),
            pl.BlockSpec((1, span), whole),
        ],
        out_specs=[
            pl.BlockSpec((1, span), whole),
            pl.BlockSpec((kept_count, BS // 2, 2 * BS), lambda i, k, c: (0, 0, 0)),
        ],
        scratch_shapes=[
            pltpu.VMEM((OV * OV, BS // 2, 2 * BS), jnp.float32),
            pltpu.VMEM((rows, rows), jnp.bfloat16),
            pltpu.VMEM((rows, rows), jnp.bfloat16),
            pltpu.VMEM((OV * OV + 1, BS // 2, 2 * BS), jnp.float32),
            pltpu.SemaphoreType.DMA((OV * OV,)),
        ],
    )
    density, pair_tiles = pl.pallas_call(
        batch_kernel,
        grid_spec=grid_spec,
        out_shape=[
            jax.ShapeDtypeStruct((1, span), jnp.float32),
            jax.ShapeDtypeStruct((kept_count, BS // 2, 2 * BS), jnp.float32),
        ],
    )(
        pick,
        code,
        grid_hi,
        grid_lo,
        permuted,
        tile_values,
        weights.reshape(1, span),
        local_pot.reshape(1, span),
    )
    return density.reshape(batch_count, points), pair_tiles


def body(coeffs, occupation, kept_tiles, tile_slot, blocks, batch_slot, tables, weights, local_pot):
    devices = lax.axis_size("tiles")
    my_index = lax.axis_index("tiles")
    kept_count = kept_tiles.shape[0]
    owned_count = kept_count // devices
    batch_count = tables.shape[0]
    batch_total = batch_slot.shape[0]
    state_count = coeffs.shape[0]
    block_total = coeffs.shape[1] // BS
    points = tables.shape[-1]
    width = OV * BS

    ladder_kept = jnp.arange(kept_count, dtype=jnp.int32)
    slot_kept = jnp.zeros((kept_count,), jnp.int32).at[tile_slot].set(ladder_kept)
    pairs = kept_tiles[slot_kept]
    partial = tile_products(coeffs, occupation, pairs).reshape(devices, owned_count, BS // 2, 2 * BS)
    owned = jnp.sum(lax.all_to_all(partial, "tiles", 0, 0, tiled=False), axis=0)
    spread = jnp.broadcast_to(owned[None], (devices, owned_count, BS // 2, 2 * BS))
    tile_values = lax.all_to_all(spread, "tiles", 0, 0, tiled=False).reshape(
        kept_count, BS // 2, 2 * BS
    )

    ladder_batch = jnp.arange(batch_total, dtype=jnp.int32)
    slot_batch = jnp.zeros((batch_total,), jnp.int32).at[batch_slot].set(ladder_batch)
    my_batches = lax.dynamic_slice_in_dim(slot_batch, my_index * batch_count, batch_count)
    my_blocks = blocks[my_batches]
    canon = jnp.sort(my_blocks[0])
    ladder_ov = jnp.arange(OV, dtype=jnp.int32)
    match = my_blocks[:, :, None] == canon[None, None, :]
    source = jnp.sum(jnp.where(match, ladder_ov[None, :, None], 0), axis=1)
    row_hit = pairs[:, 0:1] == canon[None, :]
    col_hit = pairs[:, 1:2] == canon[None, :]
    present = jnp.any(row_hit, axis=1) & jnp.any(col_hit, axis=1)
    row_place = jnp.sum(jnp.where(row_hit, ladder_ov[None, :], 0), axis=1)
    col_place = jnp.sum(jnp.where(col_hit, ladder_ov[None, :], 0), axis=1)
    pair_code = row_place * OV + col_place
    ladder_pair = jnp.arange(OV * OV, dtype=jnp.int32)
    at_pair = present[None, :] & (pair_code[None, :] == ladder_pair[:, None])
    pick = jnp.where(
        jnp.any(at_pair, axis=1), jnp.sum(jnp.where(at_pair, ladder_kept[None, :], 0), axis=1), -1
    )
    code = jnp.where(present, pair_code, OV * OV)
    after = (owned[0, 0, 0] != owned[0, 0, 0]).astype(jnp.int32)
    source = jnp.minimum(source + after, OV - 1)
    density, contrib = batch_terms(source, pick, code, tables, tile_values, weights, local_pot)

    terms = contrib.reshape(devices, owned_count, BS // 2, 2 * BS)
    matrix = jnp.sum(lax.all_to_all(terms, "tiles", 0, 0, tiled=False), axis=0)
    matrix = matrix.reshape(owned_count, BS * BS)
    return (density, matrix)


def solution(mesh):
    in_specs = (
        P(("groups", "tiles"), None),
        P(("groups", "tiles")),
        P("groups", None),
        P("groups"),
        P("groups", None),
        P("groups"),
        P(("groups", "tiles"), None, None),
        P(("groups", "tiles"), None),
        P(("groups", "tiles"), None),
    )
    out_specs = (P(("groups", "tiles"), None), P(("groups", "tiles"), None))
    return jax.shard_map(body, mesh=mesh, in_specs=in_specs, out_specs=out_specs, check_vma=False)
```

```python
import jax
import jax.numpy as jnp
from jax import lax
from jax.experimental import pallas as pl
from jax.experimental.pallas import tpu as pltpu
from jax.sharding import PartitionSpec as P

BS = 64
OV = 8


def tile_kernel(pairs_ref, *refs):
    group = (len(refs) - 2) // 2
    occ_ref = refs[2 * group]
    out_ref = refs[2 * group + 1]
    k = pl.program_id(0)
    occ_row = occ_ref[...]
    size = occ_row.shape[1]
    diagonal = lax.broadcasted_iota(jnp.int32, (size, size), 0) == lax.broadcasted_iota(jnp.int32, (size, size), 1)
    occ = jnp.sum(jnp.where(diagonal, occ_row, 0.0), axis=1, keepdims=True)
    for i in range(group):
        row_block = pairs_ref[2 * (group * k + i)]
        col_block = pairs_ref[2 * (group * k + i) + 1]
        left = refs[i][...]
        right = refs[group + i][...] * occ
        left = jnp.where(row_block % 2 == 0, left[:, :BS], left[:, BS:])
        right = jnp.where(col_block % 2 == 0, right[:, :BS], right[:, BS:])
        out_ref[i] = lax.dot_general(
            left,
            right,
            (((0,), (0,)), ((), ())),
            precision=lax.Precision.HIGHEST,
            preferred_element_type=jnp.float32,
        )


def tile_products(coeffs, occupation, pairs):
    state_count = coeffs.shape[0]
    kept_count = pairs.shape[0]
    group = next(g for g in (16, 8, 4, 2, 1) if kept_count % g == 0)

    def block_of(i, side):
        return pl.BlockSpec(
            (state_count, 2 * BS), lambda k, p: (0, p[2 * (group * k + i) + side] // 2)
        )

    grid_spec = pltpu.PrefetchScalarGridSpec(
        num_scalar_prefetch=1,
        grid=(kept_count // group,),
        in_specs=[block_of(i, 0) for i in range(group)]
        + [block_of(i, 1) for i in range(group)]
        + [pl.BlockSpec((1, state_count), lambda k, p: (0, 0))],
        out_specs=pl.BlockSpec((group, BS, BS), lambda k, p: (k, 0, 0)),
    )
    return pl.pallas_call(
        tile_kernel,
        grid_spec=grid_spec,
        out_shape=jax.ShapeDtypeStruct((kept_count, BS, BS), jnp.float32),
    )(pairs.reshape(-1), *([coeffs] * (2 * group)), occupation.reshape(1, state_count))


def split_dot(left, right, dims):
    left_hi = left.astype(jnp.bfloat16)
    left_lo = (left - left_hi.astype(jnp.float32)).astype(jnp.bfloat16)
    right_hi = right.astype(jnp.bfloat16)
    right_lo = (right - right_hi.astype(jnp.float32)).astype(jnp.bfloat16)

    def one(a, b):
        return lax.dot_general(a, b, (dims, ((), ())), preferred_element_type=jnp.float32)

    return one(left_hi, right_hi) + (one(left_hi, right_lo) + one(left_lo, right_hi))


def prep_kernel(source_ref, table_hbm, hi_ref, lo_ref, perm_ref, canon_ref, chunk_ref, table_sems, chunk_sems):
    half = BS // 2
    lane = 2 * BS
    batch_count, _, points = table_hbm.shape
    copies = []
    chunk_copies = []
    for b in range(batch_count):
        for q in range(OV):
            start = pl.multiple_of(source_ref[b * OV + q] * BS, BS)
            copy = pltpu.make_async_copy(
                table_hbm.at[b, pl.ds(start, BS), :],
                canon_ref.at[q * BS:(q + 1) * BS, b * points:(b + 1) * points],
                table_sems.at[b * OV + q],
            )
            copy.start()
            copies.append(copy)
            for h in range(points // lane):
                c = b * (points // lane) + h
                copy = pltpu.make_async_copy(
                    table_hbm.at[b, pl.ds(start, BS), h * lane:(h + 1) * lane],
                    chunk_ref.at[c, q * BS:(q + 1) * BS, :],
                    chunk_sems.at[c * OV + q],
                )
                copy.start()
                chunk_copies.append(copy)
    for copy in copies:
        copy.wait()
    grid = canon_ref[...]
    grid_hi = grid.astype(jnp.bfloat16)
    hi_ref[...] = grid_hi
    lo_ref[...] = (grid - grid_hi.astype(jnp.float32)).astype(jnp.bfloat16)
    for copy in chunk_copies:
        copy.wait()
    for c in range(chunk_ref.shape[0]):
        for q in range(OV):
            perm_ref[q * BS:q * BS + half, c * lane:(c + 1) * lane] = chunk_ref[c, pl.ds(q * BS, half, stride=2), :]
            perm_ref[q * BS + half:(q + 1) * BS, c * lane:(c + 1) * lane] = chunk_ref[
                c, pl.ds(q * BS + 1, half, stride=2), :
            ]


def prep_tables(source, tables):
    batch_count, rows, points = tables.shape
    span = batch_count * points
    whole = lambda i, s: (0, 0)
    grid_spec = pltpu.PrefetchScalarGridSpec(
        num_scalar_prefetch=1,
        grid=(1,),
        in_specs=[pl.BlockSpec(memory_space=pl.ANY)],
        out_specs=[
            pl.BlockSpec((rows, span), whole),
            pl.BlockSpec((rows, span), whole),
            pl.BlockSpec((rows, span), whole),
        ],
        scratch_shapes=[
            pltpu.VMEM((rows, span), jnp.float32),
            pltpu.VMEM((span // (2 * BS), rows, 2 * BS), jnp.float32),
            pltpu.SemaphoreType.DMA((batch_count * OV,)),
            pltpu.SemaphoreType.DMA((span // (2 * BS) * OV,)),
        ],
    )
    return pl.pallas_call(
        prep_kernel,
        grid_spec=grid_spec,
        out_shape=[
            jax.ShapeDtypeStruct((rows, span), jnp.bfloat16),
            jax.ShapeDtypeStruct((rows, span), jnp.bfloat16),
            jax.ShapeDtypeStruct((rows, span), jnp.float32),
        ],
    )(source.reshape(-1), tables)


def batch_kernel(
    pick_ref, code_ref, hi_ref, lo_ref, perm_ref, tile_hbm, weight_ref, base_ref,
    density_ref, slot_ref, stage_ref, dense_hi_ref, dense_lo_ref, pair_ref, tile_sems,
):
    half = BS // 2
    copies = []
    for p in range(OV * OV):
        copy = pltpu.make_async_copy(
            tile_hbm.at[jnp.maximum(pick_ref[p], 0)], stage_ref.at[p], tile_sems.at[p]
        )
        copy.start()
        copies.append(copy)
    for copy in copies:
        copy.wait()
    for q1 in range(OV):
        for q2 in range(OV):
            p = q1 * OV + q2
            tile = jnp.where(pick_ref[p] >= 0, stage_ref[p], 0.0)
            tile_hi = tile.astype(jnp.bfloat16)
            tile_lo = (tile - tile_hi.astype(jnp.float32)).astype(jnp.bfloat16)
            dense_hi_ref[q1 * BS:q1 * BS + half, q2 * BS:(q2 + 1) * BS] = tile_hi[:, :BS]
            dense_hi_ref[q1 * BS + half:(q1 + 1) * BS, q2 * BS:(q2 + 1) * BS] = tile_hi[:, BS:]
            dense_lo_ref[q1 * BS:q1 * BS + half, q2 * BS:(q2 + 1) * BS] = tile_lo[:, :BS]
            dense_lo_ref[q1 * BS + half:(q1 + 1) * BS, q2 * BS:(q2 + 1) * BS] = tile_lo[:, BS:]

    def dot(a, c, dims):
        return lax.dot_general(a, c, (dims, ((), ())), preferred_element_type=jnp.float32)

    grid_hi = hi_ref[...]
    grid_lo = lo_ref[...]
    dense_hi = dense_hi_ref[...]
    nn = ((1,), (0,))
    mixed = dot(dense_hi, grid_hi, nn) + (dot(dense_hi, grid_lo, nn) + dot(dense_lo_ref[...], grid_hi, nn))
    permuted = perm_ref[...]
    density = jnp.sum(permuted * mixed, axis=0, keepdims=True)
    potential = base_ref[...] + density - density * density * density / 6.0
    density_ref[...] = density
    weighted = permuted * (weight_ref[...] * potential)
    weighted_hi = weighted.astype(jnp.bfloat16)
    weighted_lo = (weighted - weighted_hi.astype(jnp.float32)).astype(jnp.bfloat16)
    nt = ((1,), (1,))
    terms = dot(weighted_hi, grid_hi, nt) + (dot(weighted_hi, grid_lo, nt) + dot(weighted_lo, grid_hi, nt))
    for q1 in range(OV):
        for q2 in range(OV):
            pair_ref[q1 * OV + q2, :, :BS] = terms[q1 * BS:q1 * BS + half, q2 * BS:(q2 + 1) * BS]
            pair_ref[q1 * OV + q2, :, BS:] = terms[q1 * BS + half:(q1 + 1) * BS, q2 * BS:(q2 + 1) * BS]
    pair_ref[OV * OV] = jnp.zeros(pair_ref.shape[1:], jnp.float32)

    def place(k, carry):
        slot_ref[k] = pair_ref[code_ref[k]]
        return carry

    lax.fori_loop(0, slot_ref.shape[0], place, 0)


def batch_terms(source, pick, code, tables, tile_values, weights, local_pot):
    batch_count, rows, points = tables.shape
    kept_count = code.shape[0]
    span = batch_count * points
    grid_hi, grid_lo, permuted = prep_tables(source, tables)
    whole = lambda i, k, c: (0, 0)
    grid_spec = pltpu.PrefetchScalarGridSpec(
        num_scalar_prefetch=2,
        grid=(1,),
        in_specs=[
            pl.BlockSpec((rows, span), whole),
            pl.BlockSpec((rows, span), whole),
            pl.BlockSpec((rows, span), whole),
            pl.BlockSpec(memory_space=pl.ANY),
            pl.BlockSpec((1, span), whole),
            pl.BlockSpec((1, span), whole),
        ],
        out_specs=[
            pl.BlockSpec((1, span), whole),
            pl.BlockSpec((kept_count, BS // 2, 2 * BS), lambda i, k, c: (0, 0, 0)),
        ],
        scratch_shapes=[
            pltpu.VMEM((OV * OV, BS // 2, 2 * BS), jnp.float32),
            pltpu.VMEM((rows, rows), jnp.bfloat16),
            pltpu.VMEM((rows, rows), jnp.bfloat16),
            pltpu.VMEM((OV * OV + 1, BS // 2, 2 * BS), jnp.float32),
            pltpu.SemaphoreType.DMA((OV * OV,)),
        ],
    )
    density, pair_tiles = pl.pallas_call(
        batch_kernel,
        grid_spec=grid_spec,
        out_shape=[
            jax.ShapeDtypeStruct((1, span), jnp.float32),
            jax.ShapeDtypeStruct((kept_count, BS // 2, 2 * BS), jnp.float32),
        ],
    )(
        pick,
        code,
        grid_hi,
        grid_lo,
        permuted,
        tile_values,
        weights.reshape(1, span),
        local_pot.reshape(1, span),
    )
    return density.reshape(batch_count, points), pair_tiles


def body(coeffs, occupation, kept_tiles, tile_slot, blocks, batch_slot, tables, weights, local_pot):
    devices = lax.axis_size("tiles")
    my_index = lax.axis_index("tiles")
    kept_count = kept_tiles.shape[0]
    owned_count = kept_count // devices
    batch_count = tables.shape[0]
    batch_total = batch_slot.shape[0]
    state_count = coeffs.shape[0]
    block_total = coeffs.shape[1] // BS
    points = tables.shape[-1]
    width = OV * BS

    ladder_kept = jnp.arange(kept_count, dtype=jnp.int32)
    slot_kept = jnp.zeros((kept_count,), jnp.int32).at[tile_slot].set(ladder_kept)
    pairs = kept_tiles[slot_kept]
    group = next(g for g in (16, 8, 4, 2, 1) if kept_count % g == 0)
    order = jnp.argsort(pairs[:, 0] * block_total + pairs[:, 1])
    layout = order.reshape(group, kept_count // group).T.reshape(-1)
    computed = tile_products(coeffs, occupation, pairs[layout])
    inverse = jnp.zeros((kept_count,), jnp.int32).at[layout].set(ladder_kept)
    partial = computed[inverse].reshape(devices, owned_count, BS // 2, 2 * BS)
    owned = jnp.sum(lax.all_to_all(partial, "tiles", 0, 0, tiled=False), axis=0)
    spread = jnp.broadcast_to(owned[None], (devices, owned_count, BS // 2, 2 * BS))
    tile_values = lax.all_to_all(spread, "tiles", 0, 0, tiled=False).reshape(
        kept_count, BS // 2, 2 * BS
    )

    ladder_batch = jnp.arange(batch_total, dtype=jnp.int32)
    slot_batch = jnp.zeros((batch_total,), jnp.int32).at[batch_slot].set(ladder_batch)
    my_batches = lax.dynamic_slice_in_dim(slot_batch, my_index * batch_count, batch_count)
    my_blocks = blocks[my_batches]
    canon = jnp.sort(my_blocks[0])
    ladder_ov = jnp.arange(OV, dtype=jnp.int32)
    match = my_blocks[:, :, None] == canon[None, None, :]
    source = jnp.sum(jnp.where(match, ladder_ov[None, :, None], 0), axis=1)
    row_hit = pairs[:, 0:1] == canon[None, :]
    col_hit = pairs[:, 1:2] == canon[None, :]
    present = jnp.any(row_hit, axis=1) & jnp.any(col_hit, axis=1)
    row_place = jnp.sum(jnp.where(row_hit, ladder_ov[None, :], 0), axis=1)
    col_place = jnp.sum(jnp.where(col_hit, ladder_ov[None, :], 0), axis=1)
    pair_code = row_place * OV + col_place
    ladder_pair = jnp.arange(OV * OV, dtype=jnp.int32)
    at_pair = present[None, :] & (pair_code[None, :] == ladder_pair[:, None])
    pick = jnp.where(
        jnp.any(at_pair, axis=1), jnp.sum(jnp.where(at_pair, ladder_kept[None, :], 0), axis=1), -1
    )
    code = jnp.where(present, pair_code, OV * OV)
    after = (owned[0, 0, 0] != owned[0, 0, 0]).astype(jnp.int32)
    source = jnp.minimum(source + after, OV - 1)
    density, contrib = batch_terms(source, pick, code, tables, tile_values, weights, local_pot)

    terms = contrib.reshape(devices, owned_count, BS // 2, 2 * BS)
    matrix = jnp.sum(lax.all_to_all(terms, "tiles", 0, 0, tiled=False), axis=0)
    matrix = matrix.reshape(owned_count, BS * BS)
    return (density, matrix)


def solution(mesh):
    in_specs = (
        P(("groups", "tiles"), None),
        P(("groups", "tiles")),
        P("groups", None),
        P("groups"),
        P("groups", None),
        P("groups"),
        P(("groups", "tiles"), None, None),
        P(("groups", "tiles"), None),
        P(("groups", "tiles"), None),
    )
    out_specs = (P(("groups", "tiles"), None), P(("groups", "tiles"), None))
    return jax.shard_map(body, mesh=mesh, in_specs=in_specs, out_specs=out_specs, check_vma=False)
```

```python
import jax
import jax.numpy as jnp
from jax import lax
from jax.experimental import pallas as pl
from jax.experimental.pallas import tpu as pltpu
from jax.sharding import PartitionSpec as P

BS = 64
OV = 8


def tile_kernel(pairs_ref, *refs):
    group = (len(refs) - 2) // 2
    occ_ref = refs[2 * group]
    out_ref = refs[2 * group + 1]
    k = pl.program_id(0)
    occ_row = occ_ref[...]
    size = occ_row.shape[1]
    diagonal = lax.broadcasted_iota(jnp.int32, (size, size), 0) == lax.broadcasted_iota(jnp.int32, (size, size), 1)
    occ = jnp.sum(jnp.where(diagonal, occ_row, 0.0), axis=1, keepdims=True)
    for i in range(group):
        row_block = pairs_ref[2 * (group * k + i)]
        col_block = pairs_ref[2 * (group * k + i) + 1]
        left = refs[i][...]
        right = refs[group + i][...] * occ
        left = jnp.where(row_block % 2 == 0, left[:, :BS], left[:, BS:])
        right = jnp.where(col_block % 2 == 0, right[:, :BS], right[:, BS:])
        out_ref[i] = split_dot(left, right, ((0,), (0,)))


def tile_products(coeffs, occupation, pairs):
    state_count = coeffs.shape[0]
    kept_count = pairs.shape[0]
    group = next(g for g in (16, 8, 4, 2, 1) if kept_count % g == 0)

    def block_of(i, side):
        return pl.BlockSpec(
            (state_count, 2 * BS), lambda k, p: (0, p[2 * (group * k + i) + side] // 2)
        )

    grid_spec = pltpu.PrefetchScalarGridSpec(
        num_scalar_prefetch=1,
        grid=(kept_count // group,),
        in_specs=[block_of(i, 0) for i in range(group)]
        + [block_of(i, 1) for i in range(group)]
        + [pl.BlockSpec((1, state_count), lambda k, p: (0, 0))],
        out_specs=pl.BlockSpec((group, BS, BS), lambda k, p: (k, 0, 0)),
    )
    return pl.pallas_call(
        tile_kernel,
        grid_spec=grid_spec,
        out_shape=jax.ShapeDtypeStruct((kept_count, BS, BS), jnp.float32),
    )(pairs.reshape(-1), *([coeffs] * (2 * group)), occupation.reshape(1, state_count))


def split_dot(left, right, dims):
    left_hi = left.astype(jnp.bfloat16)
    left_lo = (left - left_hi.astype(jnp.float32)).astype(jnp.bfloat16)
    right_hi = right.astype(jnp.bfloat16)
    right_lo = (right - right_hi.astype(jnp.float32)).astype(jnp.bfloat16)

    def one(a, b):
        return lax.dot_general(a, b, (dims, ((), ())), preferred_element_type=jnp.float32)

    return one(left_hi, right_hi) + (one(left_hi, right_lo) + one(left_lo, right_hi))


def prep_kernel(source_ref, table_hbm, hi_ref, lo_ref, perm_ref, canon_ref, chunk_ref, table_sems, chunk_sems):
    half = BS // 2
    lane = 2 * BS
    batch_count, _, points = table_hbm.shape
    copies = []
    chunk_copies = []
    for b in range(batch_count):
        for q in range(OV):
            start = pl.multiple_of(source_ref[b * OV + q] * BS, BS)
            copy = pltpu.make_async_copy(
                table_hbm.at[b, pl.ds(start, BS), :],
                canon_ref.at[q * BS:(q + 1) * BS, b * points:(b + 1) * points],
                table_sems.at[b * OV + q],
            )
            copy.start()
            copies.append(copy)
            for h in range(points // lane):
                c = b * (points // lane) + h
                copy = pltpu.make_async_copy(
                    table_hbm.at[b, pl.ds(start, BS), h * lane:(h + 1) * lane],
                    chunk_ref.at[c, q * BS:(q + 1) * BS, :],
                    chunk_sems.at[c * OV + q],
                )
                copy.start()
                chunk_copies.append(copy)
    for copy in copies:
        copy.wait()
    grid = canon_ref[...]
    grid_hi = grid.astype(jnp.bfloat16)
    hi_ref[...] = grid_hi
    lo_ref[...] = (grid - grid_hi.astype(jnp.float32)).astype(jnp.bfloat16)
    for copy in chunk_copies:
        copy.wait()
    for c in range(chunk_ref.shape[0]):
        for q in range(OV):
            perm_ref[q * BS:q * BS + half, c * lane:(c + 1) * lane] = chunk_ref[c, pl.ds(q * BS, half, stride=2), :]
            perm_ref[q * BS + half:(q + 1) * BS, c * lane:(c + 1) * lane] = chunk_ref[
                c, pl.ds(q * BS + 1, half, stride=2), :
            ]


def prep_tables(source, tables):
    batch_count, rows, points = tables.shape
    span = batch_count * points
    whole = lambda i, s: (0, 0)
    grid_spec = pltpu.PrefetchScalarGridSpec(
        num_scalar_prefetch=1,
        grid=(1,),
        in_specs=[pl.BlockSpec(memory_space=pl.ANY)],
        out_specs=[
            pl.BlockSpec((rows, span), whole),
            pl.BlockSpec((rows, span), whole),
            pl.BlockSpec((rows, span), whole),
        ],
        scratch_shapes=[
            pltpu.VMEM((rows, span), jnp.float32),
            pltpu.VMEM((span // (2 * BS), rows, 2 * BS), jnp.float32),
            pltpu.SemaphoreType.DMA((batch_count * OV,)),
            pltpu.SemaphoreType.DMA((span // (2 * BS) * OV,)),
        ],
    )
    return pl.pallas_call(
        prep_kernel,
        grid_spec=grid_spec,
        out_shape=[
            jax.ShapeDtypeStruct((rows, span), jnp.bfloat16),
            jax.ShapeDtypeStruct((rows, span), jnp.bfloat16),
            jax.ShapeDtypeStruct((rows, span), jnp.float32),
        ],
    )(source.reshape(-1), tables)


def batch_kernel(
    pick_ref, code_ref, hi_ref, lo_ref, perm_ref, tile_hbm, weight_ref, base_ref,
    density_ref, slot_ref, stage_ref, dense_hi_ref, dense_lo_ref, pair_ref, tile_sems,
):
    half = BS // 2
    copies = []
    for p in range(OV * OV):
        copy = pltpu.make_async_copy(
            tile_hbm.at[jnp.maximum(pick_ref[p], 0)], stage_ref.at[p], tile_sems.at[p]
        )
        copy.start()
        copies.append(copy)
    for copy in copies:
        copy.wait()
    for q1 in range(OV):
        for q2 in range(OV):
            p = q1 * OV + q2
            tile = jnp.where(pick_ref[p] >= 0, stage_ref[p], 0.0)
            tile_hi = tile.astype(jnp.bfloat16)
            tile_lo = (tile - tile_hi.astype(jnp.float32)).astype(jnp.bfloat16)
            dense_hi_ref[q1 * BS:q1 * BS + half, q2 * BS:(q2 + 1) * BS] = tile_hi[:, :BS]
            dense_hi_ref[q1 * BS + half:(q1 + 1) * BS, q2 * BS:(q2 + 1) * BS] = tile_hi[:, BS:]
            dense_lo_ref[q1 * BS:q1 * BS + half, q2 * BS:(q2 + 1) * BS] = tile_lo[:, :BS]
            dense_lo_ref[q1 * BS + half:(q1 + 1) * BS, q2 * BS:(q2 + 1) * BS] = tile_lo[:, BS:]

    def dot(a, c, dims):
        return lax.dot_general(a, c, (dims, ((), ())), preferred_element_type=jnp.float32)

    grid_hi = hi_ref[...]
    grid_lo = lo_ref[...]
    dense_hi = dense_hi_ref[...]
    nn = ((1,), (0,))
    mixed = dot(dense_hi, grid_hi, nn) + (dot(dense_hi, grid_lo, nn) + dot(dense_lo_ref[...], grid_hi, nn))
    permuted = perm_ref[...]
    density = jnp.sum(permuted * mixed, axis=0, keepdims=True)
    potential = base_ref[...] + density - density * density * density / 6.0
    density_ref[...] = density
    weighted = permuted * (weight_ref[...] * potential)
    weighted_hi = weighted.astype(jnp.bfloat16)
    weighted_lo = (weighted - weighted_hi.astype(jnp.float32)).astype(jnp.bfloat16)
    nt = ((1,), (1,))
    terms = dot(weighted_hi, grid_hi, nt) + (dot(weighted_hi, grid_lo, nt) + dot(weighted_lo, grid_hi, nt))
    for q1 in range(OV):
        for q2 in range(OV):
            pair_ref[q1 * OV + q2, :, :BS] = terms[q1 * BS:q1 * BS + half, q2 * BS:(q2 + 1) * BS]
            pair_ref[q1 * OV + q2, :, BS:] = terms[q1 * BS + half:(q1 + 1) * BS, q2 * BS:(q2 + 1) * BS]
    pair_ref[OV * OV] = jnp.zeros(pair_ref.shape[1:], jnp.float32)

    def place(k, carry):
        slot_ref[k] = pair_ref[code_ref[k]]
        return carry

    lax.fori_loop(0, slot_ref.shape[0], place, 0)


def batch_terms(source, pick, code, tables, tile_values, weights, local_pot):
    batch_count, rows, points = tables.shape
    kept_count = code.shape[0]
    span = batch_count * points
    grid_hi, grid_lo, permuted = prep_tables(source, tables)
    whole = lambda i, k, c: (0, 0)
    grid_spec = pltpu.PrefetchScalarGridSpec(
        num_scalar_prefetch=2,
        grid=(1,),
        in_specs=[
            pl.BlockSpec((rows, span), whole),
            pl.BlockSpec((rows, span), whole),
            pl.BlockSpec((rows, span), whole),
            pl.BlockSpec(memory_space=pl.ANY),
            pl.BlockSpec((1, span), whole),
            pl.BlockSpec((1, span), whole),
        ],
        out_specs=[
            pl.BlockSpec((1, span), whole),
            pl.BlockSpec((kept_count, BS // 2, 2 * BS), lambda i, k, c: (0, 0, 0)),
        ],
        scratch_shapes=[
            pltpu.VMEM((OV * OV, BS // 2, 2 * BS), jnp.float32),
            pltpu.VMEM((rows, rows), jnp.bfloat16),
            pltpu.VMEM((rows, rows), jnp.bfloat16),
            pltpu.VMEM((OV * OV + 1, BS // 2, 2 * BS), jnp.float32),
            pltpu.SemaphoreType.DMA((OV * OV,)),
        ],
    )
    density, pair_tiles = pl.pallas_call(
        batch_kernel,
        grid_spec=grid_spec,
        out_shape=[
            jax.ShapeDtypeStruct((1, span), jnp.float32),
            jax.ShapeDtypeStruct((kept_count, BS // 2, 2 * BS), jnp.float32),
        ],
    )(
        pick,
        code,
        grid_hi,
        grid_lo,
        permuted,
        tile_values,
        weights.reshape(1, span),
        local_pot.reshape(1, span),
    )
    return density.reshape(batch_count, points), pair_tiles


def body(coeffs, occupation, kept_tiles, tile_slot, blocks, batch_slot, tables, weights, local_pot):
    devices = lax.axis_size("tiles")
    my_index = lax.axis_index("tiles")
    kept_count = kept_tiles.shape[0]
    owned_count = kept_count // devices
    batch_count = tables.shape[0]
    batch_total = batch_slot.shape[0]
    state_count = coeffs.shape[0]
    block_total = coeffs.shape[1] // BS
    points = tables.shape[-1]
    width = OV * BS

    ladder_kept = jnp.arange(kept_count, dtype=jnp.int32)
    slot_kept = jnp.zeros((kept_count,), jnp.int32).at[tile_slot].set(ladder_kept)
    pairs = kept_tiles[slot_kept]
    partial = tile_products(coeffs, occupation, pairs).reshape(devices, owned_count, BS // 2, 2 * BS)
    owned = jnp.sum(lax.all_to_all(partial, "tiles", 0, 0, tiled=False), axis=0)
    spread = jnp.broadcast_to(owned[None], (devices, owned_count, BS // 2, 2 * BS))
    tile_values = lax.all_to_all(spread, "tiles", 0, 0, tiled=False).reshape(
        kept_count, BS // 2, 2 * BS
    )

    ladder_batch = jnp.arange(batch_total, dtype=jnp.int32)
    slot_batch = jnp.zeros((batch_total,), jnp.int32).at[batch_slot].set(ladder_batch)
    my_batches = lax.dynamic_slice_in_dim(slot_batch, my_index * batch_count, batch_count)
    my_blocks = blocks[my_batches]
    canon = jnp.sort(my_blocks[0])
    ladder_ov = jnp.arange(OV, dtype=jnp.int32)
    match = my_blocks[:, :, None] == canon[None, None, :]
    source = jnp.sum(jnp.where(match, ladder_ov[None, :, None], 0), axis=1)
    row_hit = pairs[:, 0:1] == canon[None, :]
    col_hit = pairs[:, 1:2] == canon[None, :]
    present = jnp.any(row_hit, axis=1) & jnp.any(col_hit, axis=1)
    row_place = jnp.sum(jnp.where(row_hit, ladder_ov[None, :], 0), axis=1)
    col_place = jnp.sum(jnp.where(col_hit, ladder_ov[None, :], 0), axis=1)
    pair_code = row_place * OV + col_place
    ladder_pair = jnp.arange(OV * OV, dtype=jnp.int32)
    at_pair = present[None, :] & (pair_code[None, :] == ladder_pair[:, None])
    pick = jnp.where(
        jnp.any(at_pair, axis=1), jnp.sum(jnp.where(at_pair, ladder_kept[None, :], 0), axis=1), -1
    )
    code = jnp.where(present, pair_code, OV * OV)
    after = (owned[0, 0, 0] != owned[0, 0, 0]).astype(jnp.int32)
    source = jnp.minimum(source + after, OV - 1)
    density, contrib = batch_terms(source, pick, code, tables, tile_values, weights, local_pot)

    terms = contrib.reshape(devices, owned_count, BS // 2, 2 * BS)
    matrix = jnp.sum(lax.all_to_all(terms, "tiles", 0, 0, tiled=False), axis=0)
    matrix = matrix.reshape(owned_count, BS * BS)
    return (density, matrix)


def solution(mesh):
    in_specs = (
        P(("groups", "tiles"), None),
        P(("groups", "tiles")),
        P("groups", None),
        P("groups"),
        P("groups", None),
        P("groups"),
        P(("groups", "tiles"), None, None),
        P(("groups", "tiles"), None),
        P(("groups", "tiles"), None),
    )
    out_specs = (P(("groups", "tiles"), None), P(("groups", "tiles"), None))
    return jax.shard_map(body, mesh=mesh, in_specs=in_specs, out_specs=out_specs, check_vma=False)
```
